32 devices in a mesh: groups: 2 (over x), seq: 4 (over y, core), sp: 4 (over z).
Axes of the slice: x: 2, y: 2, z: 4, core: 2. Of those that a mesh axis runs over, the one named last changes fastest.
Arguments:
- queries: bfloat16 [4096, 5120], P(('groups', 'seq', 'sp')), parts along dimension 0, may hold values from -19 to 19
- new_keys: bfloat16 [4096, 5120], P(('groups', 'seq'), 'sp'), parts along dimension 0, may hold values from -6 to 6
- new_values: bfloat16 [4096, 5120], P(('groups', 'seq'), 'sp'), parts along dimension 0, may hold values from -6 to 6
- cache_keys: bfloat16 [4096, 5120], P(('groups', 'seq'), 'sp'), parts along dimension 0, may hold values from -6 to 6
- cache_values: bfloat16 [4096, 5120], P(('groups', 'seq'), 'sp'), parts along dimension 0, may hold values from -6 to 6
- sources: int32 [8, 6], P(('groups', 'seq')), parts along dimension 0, may hold values from -1 to 7, as said below
Outputs:
- attended: bfloat16 [4096, 5120], P(('groups', 'seq', 'sp')), parts along dimension 0
The draws below stay inside these ranges and needn't reach their ends.
There are 2 independent parts, one for each index of `groups`. The reference program is written for one: setup_inputs(seed, part) draws one part's arguments, and reference() takes and returns one part's arrays. A program takes and returns all parts, laid end to end along the dimension named above; each array names one. Nothing has to cross between parts.
Inputs may be any that keep to these rules, and one draw needn't show every extreme that they name: `sources`: row q lists the 2 blocks of frame 0, then for each of 2 frames ending with the query block's own frame (frame (q + 4) // 2) its 2 blocks, or -1 for each of them where the frame lies outside the row's window or is frame 0. A window is 1 to 2 frames and always holds the own frame; all blocks of one frame share a window; entries other than -1 in a row are distinct.
All inputs are finite; a program needn't handle non-finite values.
Results may differ from the reference program's by a relative error of at most 0.006.
Values may be sent and summed in bfloat16 or wider, within the bound.
No kernel may reach another device: no remote copies, remote signals or barrier semaphores. Data moves between devices by JAX's collectives and lax.ppermute only.
A program may use at most 320 MiB of HBM per device.

```python
import jax
import jax.numpy as jnp
from jax import lax

D = 5120
HEADS = 40
HEAD_DIM = 128
BLK = 512
FB = 2
WMAX = 2
NCB = 4
NQB = 4
NB = 8
CACHE = 2048
STRETCH = 2048
LIST = 6


def drawn_pair(key):
    base = jax.random.fold_in(key, 7)
    key_rows = jnp.clip(jax.random.normal(jax.random.fold_in(base, 1), (CACHE, D), jnp.float32), -6.0, 6.0)
    query_rows = jnp.clip(jax.random.normal(jax.random.fold_in(base, 3), (STRETCH, D), jnp.float32), -6.0, 6.0)
    return (query_rows, key_rows)


def draw_queries(key, part):
    return drawn_pair(key)[0].astype(jnp.bfloat16)


def draw_cache_keys(key, part):
    return drawn_pair(key)[1].astype(jnp.bfloat16)


def draw_sources(key, part):
    frames_new = NQB // FB
    frames_old = NCB // FB
    window_span = jax.random.randint(jax.random.fold_in(key, 11), (frames_new,), 1, WMAX + 1)
    widest = jax.random.randint(jax.random.fold_in(key, 12), (), 0, frames_new)
    counter = jnp.arange(frames_new, dtype=jnp.int32)
    window_span = jnp.where(counter == widest, WMAX, window_span).astype(jnp.int32)
    frame_now = frames_old + counter
    inside = jnp.arange(FB, dtype=jnp.int32)
    columns = [jnp.broadcast_to(inside[None, :], (frames_new, FB))]
    for slot_index in range(WMAX):
        frame_at = frame_now - WMAX + 1 + slot_index
        usable = (frame_at >= frame_now - window_span + 1) & (frame_at >= 1)
        blocks_at = frame_at[:, None] * FB + inside[None, :]
        columns.append(jnp.where(usable[:, None], blocks_at, -1))
    frame_table = jnp.concatenate(columns, axis=1).astype(jnp.int32)
    return jnp.repeat(frame_table, FB, axis=0)


def steps_of(own_key, shape, shards, low, high):
    def one(position, parts):
        steps = jax.random.uniform(jax.random.fold_in(jax.random.fold_in(own_key, 6), position), (parts,), jnp.float32, low / len(shards), high / len(shards))
        return jnp.repeat(jnp.exp(steps), shape[position] // parts).reshape((-1,) + (1,) * (len(shape) - position - 1))

    gain = one(*shards[0])
    for cut in shards[1:]:
        gain = gain * one(*cut)
    return gain


def centred(rng, extent, deviation, most, cuts=(), kind=jnp.bfloat16):
    loudness = steps_of(rng, extent, cuts, -0.22, 0.18) if cuts else 1.0
    values = jax.random.normal(rng, extent, jnp.float32) * deviation * loudness
    return jnp.minimum(jnp.maximum(values, -most), most).astype(kind)


def setup_inputs(seed: int = 0, part: int = 0) -> dict:
    key_of = jax.random.split(jax.random.key(seed), 7)
    own_keys = jax.random.split(jax.random.fold_in(key_of[6], part), 7)
    return {
        "queries": draw_queries(jax.random.fold_in(jax.random.fold_in(key_of[6], part), 71), part),
        "new_keys": centred(own_keys[1], (STRETCH, D), 1.0, 6.0, ((0, 4), (1, 4))),
        "new_values": centred(own_keys[2], (STRETCH, D), 1.0, 6.0, ((0, 4), (1, 4))),
        "cache_keys": draw_cache_keys(jax.random.fold_in(jax.random.fold_in(key_of[6], part), 71), part),
        "cache_values": centred(own_keys[4], (CACHE, D), 1.0, 6.0, ((0, 4), (1, 4))),
        "sources": draw_sources(jax.random.fold_in(jax.random.fold_in(key_of[6], part), 71), part),
    }


def reference(queries, new_keys, new_values, cache_keys, cache_values, sources):
    key_all = jnp.concatenate([cache_keys, new_keys], axis=0).reshape(NB, BLK, HEADS, HEAD_DIM)
    value_all = jnp.concatenate([cache_values, new_values], axis=0).reshape(NB, BLK, HEADS, HEAD_DIM)
    query_blocks = queries.reshape(NQB, BLK, HEADS, HEAD_DIM)
    score_scale = 1.0 / (HEAD_DIM ** 0.5)

    def one_block(inputs):
        query_rows, listed = inputs
        usable = listed >= 0
        picked = jnp.where(usable, listed, 0).astype(jnp.int32)
        key_rows = key_all[picked].reshape(LIST * BLK, HEADS, HEAD_DIM).astype(jnp.float32)
        value_rows = value_all[picked].reshape(LIST * BLK, HEADS, HEAD_DIM).astype(jnp.float32)
        key_mask = jnp.repeat(usable, BLK)
        scores = jnp.einsum("qhd,khd->hqk", query_rows.astype(jnp.float32), key_rows) * score_scale
        scores = jnp.where(key_mask[None, None, :], scores, -1e30)
        largest = jnp.max(scores, axis=-1, keepdims=True)
        weights = jnp.where(key_mask[None, None, :], jnp.exp(scores - largest), 0.0)
        total = jnp.sum(weights, axis=-1)
        rounded = lax.optimization_barrier(weights.astype(jnp.bfloat16)).astype(jnp.float32)
        summed = jnp.einsum("hqk,khd->hqd", rounded, value_rows) / total[:, :, None]
        return jnp.transpose(summed, (1, 0, 2)).reshape(BLK, D).astype(jnp.bfloat16)

    result = lax.map(one_block, (query_blocks, sources))
    return result.reshape(STRETCH, D)
```

```python
import math

import jax
import jax.numpy as jnp
from jax import lax
from jax.experimental import pallas as pl
from jax.experimental.pallas import tpu as pltpu
from jax.sharding import PartitionSpec as P

HEAD_DIM = 128
NSRC = 6
ROW_SPLIT = 2


def attention_kernel(flags_ref, q_ref, *refs):
    key_refs = refs[:NSRC]
    value_refs = refs[NSRC : 2 * NSRC]
    out_ref = refs[2 * NSRC]
    score_ref = refs[2 * NSRC + 1]
    score_scale = 1.0 / math.sqrt(HEAD_DIM)
    query = q_ref[...]
    top = None
    for j in range(NSRC):
        scores = lax.dot_general(
            query, key_refs[j][...], (((1,), (1,)), ((), ())), preferred_element_type=jnp.float32
        ) * score_scale
        scores = jnp.where(flags_ref[j] > 0, scores, -1e30)
        score_ref[j] = scores
        block_top = jnp.max(scores, axis=1, keepdims=True)
        top = block_top if top is None else jnp.maximum(top, block_top)
    total = None
    summed = None
    for j in range(NSRC):
        weights = jnp.exp(score_ref[j] - top)
        part_total = jnp.sum(weights, axis=1, keepdims=True)
        product = jnp.dot(
            weights.astype(jnp.bfloat16), value_refs[j][...], preferred_element_type=jnp.float32
        )
        total = part_total if total is None else total + part_total
        summed = product if summed is None else summed + product
    out_ref[...] = (summed / total).astype(out_ref.dtype)


def attend(flags, query_block, key_blocks, value_blocks):
    rows, width = query_block.shape
    block_rows = key_blocks[0].shape[0]
    nheads = width // HEAD_DIM
    row_tile = rows // ROW_SPLIT
    q_spec = pl.BlockSpec((row_tile, HEAD_DIM), lambda h, r, f: (r, h))
    kv_spec = pl.BlockSpec((block_rows, HEAD_DIM), lambda h, r, f: (0, h))
    grid_spec = pltpu.PrefetchScalarGridSpec(
        num_scalar_prefetch=1,
        grid=(nheads, ROW_SPLIT),
        in_specs=[q_spec] + [kv_spec] * (2 * NSRC),
        out_specs=q_spec,
        scratch_shapes=[pltpu.VMEM((NSRC, row_tile, block_rows), jnp.float32)],
    )
    return pl.pallas_call(
        attention_kernel,
        grid_spec=grid_spec,
        out_shape=jax.ShapeDtypeStruct((rows, width), jnp.bfloat16),
        compiler_params=pltpu.CompilerParams(dimension_semantics=("parallel", "arbitrary")),
    )(flags, query_block, *key_blocks, *value_blocks)


def local(queries, new_keys, new_values, cache_keys, cache_values, sources):
    head_width = new_keys.shape[1]
    sp_count = lax.axis_size("sp")
    sp_place = lax.axis_index("sp")
    seq_count = lax.axis_size("seq")
    seq_place = lax.axis_index("seq")
    chips = seq_count // 2

    query_parts = [lax.dynamic_slice_in_dim(queries, sp_place * head_width, head_width, 1)]
    for d in range(1, sp_count):
        columns = ((sp_place + d) % sp_count) * head_width
        piece = lax.dynamic_slice_in_dim(queries, columns, head_width, 1)
        query_parts.append(
            lax.ppermute(piece, "sp", [(i, (i + d) % sp_count) for i in range(sp_count)])
        )
    query_block = jnp.concatenate(query_parts, axis=0)

    swap = [(i, i ^ 1) for i in range(seq_count)]
    partner = lax.ppermute((new_keys, new_values), "seq", swap)

    first = (cache_keys, cache_values)
    span = 1
    while span < chips:
        pairs = [
            (2 * c + k, 2 * (c + span) + k)
            for c in range(span)
            if c + span < chips
            for k in range(2)
        ]
        got = lax.ppermute(first, "seq", pairs)
        chip = seq_place // 2
        taking = (chip >= span) & (chip < 2 * span)
        first = tuple(jnp.where(taking, b, a) for a, b in zip(first, got))
        span *= 2

    last_chip = seq_place >= seq_count - 2
    sending = tuple(
        jnp.where(last_chip, c, n) for c, n in zip((cache_keys, cache_values), (new_keys, new_values))
    )
    before = lax.ppermute(sending, "seq", [(i, (i + 2) % seq_count) for i in range(seq_count)])

    first_other, before_other = lax.ppermute((first, before), "seq", swap)

    other = seq_place ^ 1
    block_ids = jnp.stack(
        [
            seq_count + seq_place,
            seq_count + other,
            seq_place % 2,
            other % 2,
            seq_count + seq_place - 2,
            seq_count + other - 2,
        ]
    ).astype(jnp.int32)
    listed = sources[0]
    flags = jnp.any(listed[None, :] == block_ids[:, None], axis=1).astype(jnp.int32)

    held = [(new_keys, new_values), partner, first, first_other, before, before_other]
    heads_out = attend(flags, query_block, [k for k, _ in held], [v for _, v in held])

    rows = queries.shape[0]
    result = jnp.zeros((rows, queries.shape[1]), jnp.bfloat16)
    for d in range(sp_count):
        piece = heads_out[d * rows : (d + 1) * rows]
        if d:
            piece = lax.ppermute(piece, "sp", [(i, (i - d) % sp_count) for i in range(sp_count)])
        columns = ((sp_place + d) % sp_count) * head_width
        result = lax.dynamic_update_slice_in_dim(result, piece, columns, 1)
    return result


def solution(mesh):
    return jax.shard_map(
        local,
        mesh=mesh,
        in_specs=(
            P(("groups", "seq", "sp"), None),
            P(("groups", "seq"), "sp"),
            P(("groups", "seq"), "sp"),
            P(("groups", "seq"), "sp"),
            P(("groups", "seq"), "sp"),
            P(("groups", "seq"), None),
        ),
        out_specs=P(("groups", "seq", "sp"), None),
        check_vma=False,
    )
```

```python
import math

import jax
import jax.numpy as jnp
from jax import lax
from jax.experimental import pallas as pl
from jax.experimental.pallas import tpu as pltpu
from jax.sharding import PartitionSpec as P

HEAD_DIM = 128
ROW_SPLIT = 2
STAT_ROWS = 8


def partial_kernel(nsrc, flags_ref, q_ref, *refs):
    key_refs = refs[:nsrc]
    value_refs = refs[nsrc : 2 * nsrc]
    out_ref, lse_ref = refs[2 * nsrc : 2 * nsrc + 2]
    score_ref, top_ref, total_ref, summed_ref = refs[2 * nsrc + 2 :]
    score_scale = 1.0 / math.sqrt(HEAD_DIM)
    query = q_ref[...]
    top_ref[...] = jnp.full(top_ref.shape, -1e30, jnp.float32)
    total_ref[...] = jnp.zeros(total_ref.shape, jnp.float32)
    summed_ref[...] = jnp.zeros(summed_ref.shape, jnp.float32)
    for j in range(nsrc):

        @pl.when(flags_ref[j] > 0)
        def _():
            scores = lax.dot_general(
                query, key_refs[j][...], (((1,), (1,)), ((), ())), preferred_element_type=jnp.float32
            ) * score_scale
            score_ref[j] = scores
            top_ref[...] = jnp.maximum(top_ref[...], jnp.max(scores, axis=1, keepdims=True))

    for j in range(nsrc):

        @pl.when(flags_ref[j] > 0)
        def _():
            weights = jnp.exp(score_ref[j] - top_ref[...])
            total_ref[...] += jnp.sum(weights, axis=1, keepdims=True)
            summed_ref[...] += jnp.dot(
                weights.astype(jnp.bfloat16), value_refs[j][...], preferred_element_type=jnp.float32
            )

    total = total_ref[...]
    filled = total > 0
    safe = jnp.where(filled, total, 1.0)
    out_ref[...] = jnp.where(filled, summed_ref[...] / safe, 0.0).astype(out_ref.dtype)
    lse = jnp.where(filled, top_ref[...] + jnp.log(safe), -1e30)
    wide = jnp.broadcast_to(lse, (lse.shape[0], 128))
    lse_ref[...] = jnp.transpose(wide)[:STAT_ROWS]


def attend_partial(flags, query_block, key_blocks, value_blocks, out_dtype):
    nsrc = len(key_blocks)
    rows, width = query_block.shape
    block_rows = key_blocks[0].shape[0]
    nheads = width // HEAD_DIM
    row_tile = rows // ROW_SPLIT
    q_spec = pl.BlockSpec((row_tile, HEAD_DIM), lambda h, r, f: (r, h))
    kv_spec = pl.BlockSpec((block_rows, HEAD_DIM), lambda h, r, f: (0, h))
    lse_spec = pl.BlockSpec((None, STAT_ROWS, row_tile), lambda h, r, f: (h, 0, r))
    grid_spec = pltpu.PrefetchScalarGridSpec(
        num_scalar_prefetch=1,
        grid=(nheads, ROW_SPLIT),
        in_specs=[q_spec] + [kv_spec] * (2 * nsrc),
        out_specs=[q_spec, lse_spec],
        scratch_shapes=[
            pltpu.VMEM((nsrc, row_tile, block_rows), jnp.float32),
            pltpu.VMEM((row_tile, 1), jnp.float32),
            pltpu.VMEM((row_tile, 1), jnp.float32),
            pltpu.VMEM((row_tile, HEAD_DIM), jnp.float32),
        ],
    )
    return pl.pallas_call(
        lambda *a: partial_kernel(nsrc, *a),
        grid_spec=grid_spec,
        out_shape=[
            jax.ShapeDtypeStruct((rows, width), out_dtype),
            jax.ShapeDtypeStruct((nheads, STAT_ROWS, rows), jnp.float32),
        ],
        compiler_params=pltpu.CompilerParams(dimension_semantics=("parallel", "arbitrary")),
    )(flags, query_block, *key_blocks, *value_blocks)


def membership(listed, block_ids, valid):
    hit = jnp.any(listed[None, :] == jnp.stack(block_ids)[:, None], axis=1)
    return (hit & jnp.stack(valid)).astype(jnp.int32)


def local(queries, new_keys, new_values, cache_keys, cache_values, sources):
    head_width = new_keys.shape[1]
    nheads = head_width // HEAD_DIM
    sp_count = lax.axis_size("sp")
    sp_place = lax.axis_index("sp")
    seq_count = lax.axis_size("seq")
    s = lax.axis_index("seq")
    chips = seq_count // 2
    chip = s // 2
    other = s ^ 1
    listed = sources[0]

    query_parts = [lax.dynamic_slice_in_dim(queries, sp_place * head_width, head_width, 1)]
    for d in range(1, sp_count):
        columns = ((sp_place + d) % sp_count) * head_width
        piece = lax.dynamic_slice_in_dim(queries, columns, head_width, 1)
        query_parts.append(
            lax.ppermute(piece, "sp", [(i, (i + d) % sp_count) for i in range(sp_count)])
        )
    query_block = jnp.concatenate(query_parts, axis=0)

    back = [(i, (i - 2) % seq_count) for i in range(seq_count)]
    forth = [(i, (i + 2) % seq_count) for i in range(seq_count)]
    t = (s - 2) % seq_count
    t_chip = t // 2
    remote_ids = [seq_count + t, seq_count + (t ^ 1), t, t ^ 1]
    remote_valid = [
        s >= 2,
        s >= 2,
        (t_chip == 0) | (t_chip == chips - 1),
        (t_chip == 0) | (t_chip == chips - 1),
    ]
    if chips > 2:
        remote_ids += [t % 2, 1 - t % 2]
        remote_valid += [(t_chip >= 1) & (t_chip <= chips - 2)] * 2
    remote_flags = membership(listed, remote_ids, remote_valid)
    got_query, got_flags = lax.ppermute((query_block, remote_flags), "seq", back)

    swap = [(i, i ^ 1) for i in range(seq_count)]
    partner_k, partner_v, partner_ck, partner_cv = lax.ppermute(
        (new_keys, new_values, cache_keys, cache_values), "seq", swap
    )
    keys = [new_keys, partner_k, cache_keys, partner_ck]
    values = [new_values, partner_v, cache_values, partner_cv]

    if chips > 2:
        first = (cache_keys, cache_values)
        span = 1
        while span < chips - 1:
            pairs = [
                (2 * c + k, 2 * (c + span) + k)
                for c in range(span)
                if c + span < chips - 1
                for k in range(2)
            ]
            got = lax.ppermute(first, "seq", pairs)
            taking = (chip >= span) & (chip < 2 * span)
            first = tuple(jnp.where(taking, b, a) for a, b in zip(first, got))
            span *= 2
        first_other = lax.ppermute(first, "seq", swap)
        remote_keys = keys + [first[0], first_other[0]]
        remote_values = values + [first[1], first_other[1]]
    else:
        remote_keys, remote_values = keys, values

    local_flags = membership(
        listed,
        [seq_count + s, seq_count + other, s, other],
        [s >= 0, s >= 0, chip == 0, chip == 0],
    )
    local_out, local_lse = attend_partial(local_flags, query_block, keys, values, jnp.float32)

    far_out, far_lse = attend_partial(got_flags, got_query, remote_keys, remote_values, jnp.bfloat16)
    far_out, far_lse = lax.ppermute((far_out, far_lse), "seq", forth)

    rows_all = query_block.shape[0]
    lse_a = local_lse[:, 0, :].T[:, :, None]
    lse_b = far_lse[:, 0, :].T[:, :, None]
    top = jnp.maximum(lse_a, lse_b)
    weight_a = jnp.exp(lse_a - top)
    weight_b = jnp.exp(lse_b - top)
    mixed = (
        local_out.reshape(rows_all, nheads, HEAD_DIM) * weight_a
        + far_out.astype(jnp.float32).reshape(rows_all, nheads, HEAD_DIM) * weight_b
    ) / (weight_a + weight_b)
    heads_out = mixed.reshape(rows_all, head_width).astype(jnp.bfloat16)

    rows = queries.shape[0]
    result = jnp.zeros((rows, queries.shape[1]), jnp.bfloat16)
    for d in range(sp_count):
        piece = heads_out[d * rows : (d + 1) * rows]
        if d:
            piece = lax.ppermute(piece, "sp", [(i, (i - d) % sp_count) for i in range(sp_count)])
        columns = ((sp_place + d) % sp_count) * head_width
        result = lax.dynamic_update_slice_in_dim(result, piece, columns, 1)
    return result


def solution(mesh):
    return jax.shard_map(
        local,
        mesh=mesh,
        in_specs=(
            P(("groups", "seq", "sp"), None),
            P(("groups", "seq"), "sp"),
            P(("groups", "seq"), "sp"),
            P(("groups", "seq"), "sp"),
            P(("groups", "seq"), "sp"),
            P(("groups", "seq"), None),
        ),
        out_specs=P(("groups", "seq", "sp"), None),
        check_vma=False,
    )
```

```python
import math

import jax
import jax.numpy as jnp
from jax import lax
from jax.experimental import pallas as pl
from jax.experimental.pallas import tpu as pltpu
from jax.sharding import PartitionSpec as P

HEAD_DIM = 128
ROW_SPLIT = 2
STAT_ROWS = 8


def partial_kernel(nsrc, flags_ref, q_ref, *refs):
    key_refs = refs[:nsrc]
    value_refs = refs[nsrc : 2 * nsrc]
    out_ref, lse_ref = refs[2 * nsrc : 2 * nsrc + 2]
    score_ref = refs[2 * nsrc + 2]
    score_scale = 1.0 / math.sqrt(HEAD_DIM)
    query = q_ref[...]
    top = None
    for j in range(nsrc):
        scores = lax.dot_general(
            query, key_refs[j][...], (((1,), (1,)), ((), ())), preferred_element_type=jnp.float32
        ) * score_scale
        scores = jnp.where(flags_ref[j] > 0, scores, -1e30)
        score_ref[j] = scores
        block_top = jnp.max(scores, axis=1, keepdims=True)
        top = block_top if top is None else jnp.maximum(top, block_top)
    total = None
    summed = None
    for j in range(nsrc):
        weights = jnp.exp(score_ref[j] - top)
        part_total = jnp.sum(weights, axis=1, keepdims=True)
        product = jnp.dot(
            weights.astype(jnp.bfloat16), value_refs[j][...], preferred_element_type=jnp.float32
        )
        total = part_total if total is None else total + part_total
        summed = product if summed is None else summed + product
    out_ref[...] = (summed / total).astype(out_ref.dtype)
    lse = top + jnp.log(total)
    wide = jnp.broadcast_to(lse, (lse.shape[0], 128))
    lse_ref[...] = jnp.transpose(wide)[:STAT_ROWS]


def attend_partial(flags, query_block, key_blocks, value_blocks, out_dtype):
    nsrc = len(key_blocks)
    rows, width = query_block.shape
    block_rows = key_blocks[0].shape[0]
    nheads = width // HEAD_DIM
    row_tile = rows // ROW_SPLIT
    q_spec = pl.BlockSpec((row_tile, HEAD_DIM), lambda h, r, f: (r, h))
    kv_spec = pl.BlockSpec((block_rows, HEAD_DIM), lambda h, r, f: (0, h))
    lse_spec = pl.BlockSpec((None, STAT_ROWS, row_tile), lambda h, r, f: (h, 0, r))
    grid_spec = pltpu.PrefetchScalarGridSpec(
        num_scalar_prefetch=1,
        grid=(nheads, ROW_SPLIT),
        in_specs=[q_spec] + [kv_spec] * (2 * nsrc),
        out_specs=[q_spec, lse_spec],
        scratch_shapes=[pltpu.VMEM((nsrc, row_tile, block_rows), jnp.float32)],
    )
    return pl.pallas_call(
        lambda *a: partial_kernel(nsrc, *a),
        grid_spec=grid_spec,
        out_shape=[
            jax.ShapeDtypeStruct((rows, width), out_dtype),
            jax.ShapeDtypeStruct((nheads, STAT_ROWS, rows), jnp.float32),
        ],
        compiler_params=pltpu.CompilerParams(dimension_semantics=("parallel", "arbitrary")),
    )(flags, query_block, *key_blocks, *value_blocks)


def membership(listed, block_ids, valid):
    hit = jnp.any(listed[None, :] == jnp.stack(block_ids)[:, None], axis=1)
    return (hit & jnp.stack(valid)).astype(jnp.int32)


def local(queries, new_keys, new_values, cache_keys, cache_values, sources):
    head_width = new_keys.shape[1]
    nheads = head_width // HEAD_DIM
    sp_count = lax.axis_size("sp")
    sp_place = lax.axis_index("sp")
    seq_count = lax.axis_size("seq")
    s = lax.axis_index("seq")
    chips = seq_count // 2
    chip = s // 2
    other = s ^ 1
    listed = sources[0]

    query_parts = [lax.dynamic_slice_in_dim(queries, sp_place * head_width, head_width, 1)]
    for d in range(1, sp_count):
        columns = ((sp_place + d) % sp_count) * head_width
        piece = lax.dynamic_slice_in_dim(queries, columns, head_width, 1)
        query_parts.append(
            lax.ppermute(piece, "sp", [(i, (i + d) % sp_count) for i in range(sp_count)])
        )
    query_block = jnp.concatenate(query_parts, axis=0)

    back = [(i, (i - 2) % seq_count) for i in range(seq_count)]
    forth = [(i, (i + 2) % seq_count) for i in range(seq_count)]
    t = (s - 2) % seq_count
    t_chip = t // 2
    remote_ids = [seq_count + t, seq_count + (t ^ 1), t, t ^ 1]
    remote_valid = [
        s >= 2,
        s >= 2,
        (t_chip == 0) | (t_chip == chips - 1),
        (t_chip == 0) | (t_chip == chips - 1),
    ]
    if chips > 2:
        remote_ids += [t % 2, 1 - t % 2]
        remote_valid += [(t_chip >= 1) & (t_chip <= chips - 2)] * 2
    remote_flags = membership(listed, remote_ids, remote_valid)
    got_query, got_flags = lax.ppermute((query_block, remote_flags), "seq", back)

    swap = [(i, i ^ 1) for i in range(seq_count)]
    partner_k, partner_v, partner_ck, partner_cv = lax.ppermute(
        (new_keys, new_values, cache_keys, cache_values), "seq", swap
    )
    keys = [new_keys, partner_k, cache_keys, partner_ck]
    values = [new_values, partner_v, cache_values, partner_cv]

    if chips > 2:
        first = (cache_keys, cache_values)
        span = 1
        while span < chips - 1:
            pairs = [
                (2 * c + k, 2 * (c + span) + k)
                for c in range(span)
                if c + span < chips - 1
                for k in range(2)
            ]
            got = lax.ppermute(first, "seq", pairs)
            taking = (chip >= span) & (chip < 2 * span)
            first = tuple(jnp.where(taking, b, a) for a, b in zip(first, got))
            span *= 2
        first_other = lax.ppermute(first, "seq", swap)
        remote_keys = keys + [first[0], first_other[0]]
        remote_values = values + [first[1], first_other[1]]
    else:
        remote_keys, remote_values = keys, values

    local_flags = membership(
        listed,
        [seq_count + s, seq_count + other, s, other],
        [s >= 0, s >= 0, chip == 0, chip == 0],
    )
    local_out, local_lse = attend_partial(local_flags, query_block, keys, values, jnp.float32)

    far_out, far_lse = attend_partial(got_flags, got_query, remote_keys, remote_values, jnp.bfloat16)
    far_out, far_lse = lax.ppermute((far_out, far_lse), "seq", forth)

    rows_all = query_block.shape[0]
    lse_a = local_lse[:, 0, :].T
    lse_b = far_lse[:, 0, :].T
    top = jnp.maximum(lse_a, lse_b)
    weight_a = jnp.repeat(jnp.exp(lse_a - top), HEAD_DIM, axis=1)
    weight_b = jnp.repeat(jnp.exp(lse_b - top), HEAD_DIM, axis=1)
    mixed = (local_out * weight_a + far_out.astype(jnp.float32) * weight_b) / (weight_a + weight_b)
    heads_out = mixed.astype(jnp.bfloat16)

    rows = queries.shape[0]
    result = jnp.zeros((rows, queries.shape[1]), jnp.bfloat16)
    for d in range(sp_count):
        piece = heads_out[d * rows : (d + 1) * rows]
        if d:
            piece = lax.ppermute(piece, "sp", [(i, (i - d) % sp_count) for i in range(sp_count)])
        columns = ((sp_place + d) % sp_count) * head_width
        result = lax.dynamic_update_slice_in_dim(result, piece, columns, 1)
    return result


def solution(mesh):
    return jax.shard_map(
        local,
        mesh=mesh,
        in_specs=(
            P(("groups", "seq", "sp"), None),
            P(("groups", "seq"), "sp"),
            P(("groups", "seq"), "sp"),
            P(("groups", "seq"), "sp"),
            P(("groups", "seq"), "sp"),
            P(("groups", "seq"), None),
        ),
        out_specs=P(("groups", "seq", "sp"), None),
        check_vma=False,
    )
```

```python
import math

import jax
import jax.numpy as jnp
from jax import lax
from jax.experimental import pallas as pl
from jax.experimental.pallas import tpu as pltpu
from jax.sharding import PartitionSpec as P

HEAD_DIM = 128
ROW_SPLIT = 1
STAT_ROWS = 8


def partial_kernel(nsrc, flags_ref, q_ref, *refs):
    key_refs = refs[:nsrc]
    value_refs = refs[nsrc : 2 * nsrc]
    out_ref, lse_ref = refs[2 * nsrc : 2 * nsrc + 2]
    score_ref = refs[2 * nsrc + 2]
    score_scale = 1.0 / math.sqrt(HEAD_DIM)
    query = q_ref[...]
    top = None
    for j in range(nsrc):
        scores = lax.dot_general(
            query, key_refs[j][...], (((1,), (1,)), ((), ())), preferred_element_type=jnp.float32
        ) * score_scale
        scores = jnp.where(flags_ref[j] > 0, scores, -1e30)
        score_ref[j] = scores
        block_top = jnp.max(scores, axis=1, keepdims=True)
        top = block_top if top is None else jnp.maximum(top, block_top)
    total = None
    summed = None
    for j in range(nsrc):
        weights = jnp.exp(score_ref[j] - top)
        part_total = jnp.sum(weights, axis=1, keepdims=True)
        product = jnp.dot(
            weights.astype(jnp.bfloat16), value_refs[j][...], preferred_element_type=jnp.float32
        )
        total = part_total if total is None else total + part_total
        summed = product if summed is None else summed + product
    out_ref[...] = (summed / total).astype(out_ref.dtype)
    lse = top + jnp.log(total)
    wide = jnp.broadcast_to(lse, (lse.shape[0], 128))
    lse_ref[...] = jnp.transpose(wide)[:STAT_ROWS]


def attend_partial(flags, query_block, key_blocks, value_blocks, out_dtype):
    nsrc = len(key_blocks)
    rows, width = query_block.shape
    block_rows = key_blocks[0].shape[0]
    nheads = width // HEAD_DIM
    row_tile = rows // ROW_SPLIT
    q_spec = pl.BlockSpec((row_tile, HEAD_DIM), lambda h, r, f: (r, h))
    kv_spec = pl.BlockSpec((block_rows, HEAD_DIM), lambda h, r, f: (0, h))
    lse_spec = pl.BlockSpec((None, STAT_ROWS, row_tile), lambda h, r, f: (h, 0, r))
    grid_spec = pltpu.PrefetchScalarGridSpec(
        num_scalar_prefetch=1,
        grid=(nheads, ROW_SPLIT),
        in_specs=[q_spec] + [kv_spec] * (2 * nsrc),
        out_specs=[q_spec, lse_spec],
        scratch_shapes=[pltpu.VMEM((nsrc, row_tile, block_rows), jnp.float32)],
    )
    return pl.pallas_call(
        lambda *a: partial_kernel(nsrc, *a),
        grid_spec=grid_spec,
        out_shape=[
            jax.ShapeDtypeStruct((rows, width), out_dtype),
            jax.ShapeDtypeStruct((nheads, STAT_ROWS, rows), jnp.float32),
        ],
        compiler_params=pltpu.CompilerParams(dimension_semantics=("parallel", "arbitrary")),
    )(flags, query_block, *key_blocks, *value_blocks)


def membership(listed, block_ids, valid):
    hit = jnp.any(listed[None, :] == jnp.stack(block_ids)[:, None], axis=1)
    return (hit & jnp.stack(valid)).astype(jnp.int32)


def local(queries, new_keys, new_values, cache_keys, cache_values, sources):
    head_width = new_keys.shape[1]
    nheads = head_width // HEAD_DIM
    sp_count = lax.axis_size("sp")
    sp_place = lax.axis_index("sp")
    seq_count = lax.axis_size("seq")
    s = lax.axis_index("seq")
    chips = seq_count // 2
    chip = s // 2
    other = s ^ 1
    listed = sources[0]

    rows = queries.shape[0]
    back = [(i, (i - 2) % seq_count) for i in range(seq_count)]
    forth = [(i, (i + 2) % seq_count) for i in range(seq_count)]
    t = (s - 2) % seq_count
    t_chip = t // 2
    remote_ids = [seq_count + t, seq_count + (t ^ 1), t, t ^ 1]
    remote_valid = [
        s >= 2,
        s >= 2,
        (t_chip == 0) | (t_chip == chips - 1),
        (t_chip == 0) | (t_chip == chips - 1),
    ]
    if chips > 2:
        remote_ids += [t % 2, 1 - t % 2]
        remote_valid += [(t_chip >= 1) & (t_chip <= chips - 2)] * 2
    remote_flags = membership(listed, remote_ids, remote_valid)
    got_flags = lax.ppermute(remote_flags, "seq", back)

    swap = [(i, i ^ 1) for i in range(seq_count)]
    partner_k, partner_v, partner_ck, partner_cv = lax.ppermute(
        (new_keys, new_values, cache_keys, cache_values), "seq", swap
    )
    keys = [new_keys, partner_k, cache_keys, partner_ck]
    values = [new_values, partner_v, cache_values, partner_cv]

    if chips > 2:
        first = (cache_keys, cache_values)
        span = 1
        while span < chips - 1:
            pairs = [
                (2 * c + k, 2 * (c + span) + k)
                for c in range(span)
                if c + span < chips - 1
                for k in range(2)
            ]
            got = lax.ppermute(first, "seq", pairs)
            taking = (chip >= span) & (chip < 2 * span)
            first = tuple(jnp.where(taking, b, a) for a, b in zip(first, got))
            span *= 2
        first_other = lax.ppermute(first, "seq", swap)
        remote_keys = keys + [first[0], first_other[0]]
        remote_values = values + [first[1], first_other[1]]
    else:
        remote_keys, remote_values = keys, values

    local_flags = membership(
        listed,
        [seq_count + s, seq_count + other, s, other],
        [s >= 0, s >= 0, chip == 0, chip == 0],
    )

    result = jnp.zeros((rows, queries.shape[1]), jnp.bfloat16)
    for d in range(sp_count):
        columns = ((sp_place + d) % sp_count) * head_width
        chunk = lax.dynamic_slice_in_dim(queries, columns, head_width, 1)
        if d:
            chunk = lax.ppermute(chunk, "sp", [(i, (i + d) % sp_count) for i in range(sp_count)])
        got_chunk = lax.ppermute(chunk, "seq", back)
        local_out, local_lse = attend_partial(local_flags, chunk, keys, values, jnp.float32)
        far_out, far_lse = attend_partial(
            got_flags, got_chunk, remote_keys, remote_values, jnp.bfloat16
        )
        far_out, far_lse = lax.ppermute((far_out, far_lse), "seq", forth)
        lse_a = local_lse[:, 0, :].T
        lse_b = far_lse[:, 0, :].T
        top = jnp.maximum(lse_a, lse_b)
        weight_a = jnp.repeat(jnp.exp(lse_a - top), HEAD_DIM, axis=1)
        weight_b = jnp.repeat(jnp.exp(lse_b - top), HEAD_DIM, axis=1)
        mixed = (local_out * weight_a + far_out.astype(jnp.float32) * weight_b) / (
            weight_a + weight_b
        )
        piece = mixed.astype(jnp.bfloat16)
        if d:
            piece = lax.ppermute(piece, "sp", [(i, (i - d) % sp_count) for i in range(sp_count)])
        columns = ((sp_place + d) % sp_count) * head_width
        result = lax.dynamic_update_slice_in_dim(result, piece, columns, 1)
    return result


def solution(mesh):
    return jax.shard_map(
        local,
        mesh=mesh,
        in_specs=(
            P(("groups", "seq", "sp"), None),
            P(("groups", "seq"), "sp"),
            P(("groups", "seq"), "sp"),
            P(("groups", "seq"), "sp"),
            P(("groups", "seq"), "sp"),
            P(("groups", "seq"), None),
        ),
        out_specs=P(("groups", "seq", "sp"), None),
        check_vma=False,
    )
```

```python
import math

import jax
import jax.numpy as jnp
from jax import lax
from jax.experimental import pallas as pl
from jax.experimental.pallas import tpu as pltpu
from jax.sharding import PartitionSpec as P

HEAD_DIM = 128
ROW_SPLIT = 1
STAT_ROWS = 8


def partial_kernel(nsrc, flags_ref, q_ref, *refs):
    key_refs = refs[:nsrc]
    value_refs = refs[nsrc : 2 * nsrc]
    out_ref, lse_ref = refs[2 * nsrc : 2 * nsrc + 2]
    score_scale = 1.0 / math.sqrt(HEAD_DIM)
    query = q_ref[...]

    def raw_scores(j):
        return lax.dot_general(
            query, key_refs[j][...], (((1,), (1,)), ((), ())), preferred_element_type=jnp.float32
        )

    top = None
    for j in range(nsrc):
        block_top = jnp.max(raw_scores(j), axis=1, keepdims=True)
        block_top = jnp.where(flags_ref[j] > 0, block_top, -1e30)
        top = block_top if top is None else jnp.maximum(top, block_top)
    top = top * score_scale
    total = None
    summed = None
    for j in range(nsrc):
        shift = jnp.where(flags_ref[j] > 0, top, 1e30)
        weights = jnp.exp(raw_scores(j) * score_scale - shift)
        part_total = jnp.sum(weights, axis=1, keepdims=True)
        product = jnp.dot(
            weights.astype(jnp.bfloat16), value_refs[j][...], preferred_element_type=jnp.float32
        )
        total = part_total if total is None else total + part_total
        summed = product if summed is None else summed + product
    filled = total > 0
    safe = jnp.where(filled, total, 1.0)
    out_ref[...] = (summed / safe).astype(out_ref.dtype)
    lse = jnp.where(filled, top + jnp.log(safe), -1e30)
    wide = jnp.broadcast_to(lse, (lse.shape[0], 128))
    lse_ref[...] = jnp.transpose(wide)[:STAT_ROWS]


def attend_partial(flags, query_block, key_blocks, value_blocks, out_dtype):
    nsrc = len(key_blocks)
    rows, width = query_block.shape
    block_rows = key_blocks[0].shape[0]
    nheads = width // HEAD_DIM
    row_tile = rows // ROW_SPLIT
    q_spec = pl.BlockSpec((row_tile, HEAD_DIM), lambda h, r, f: (r, h))
    kv_spec = pl.BlockSpec((block_rows, HEAD_DIM), lambda h, r, f: (0, h))
    out_spec = pl.BlockSpec((None, row_tile, HEAD_DIM), lambda h, r, f: (h, r, 0))
    lse_spec = pl.BlockSpec((None, STAT_ROWS, row_tile), lambda h, r, f: (h, 0, r))
    grid_spec = pltpu.PrefetchScalarGridSpec(
        num_scalar_prefetch=1,
        grid=(nheads, ROW_SPLIT),
        in_specs=[q_spec] + [kv_spec] * (2 * nsrc),
        out_specs=[out_spec, lse_spec],
    )
    return pl.pallas_call(
        lambda *a: partial_kernel(nsrc, *a),
        grid_spec=grid_spec,
        out_shape=[
            jax.ShapeDtypeStruct((nheads, rows, HEAD_DIM), out_dtype),
            jax.ShapeDtypeStruct((nheads, STAT_ROWS, rows), jnp.float32),
        ],
        compiler_params=pltpu.CompilerParams(dimension_semantics=("parallel", "arbitrary")),
    )(flags, query_block, *key_blocks, *value_blocks)


def membership(listed, block_ids, valid):
    hit = jnp.any(listed[None, :] == jnp.stack(block_ids)[:, None], axis=1)
    return (hit & jnp.stack(valid)).astype(jnp.int32)


def local(queries, new_keys, new_values, cache_keys, cache_values, sources):
    head_width = new_keys.shape[1]
    nheads = head_width // HEAD_DIM
    sp_count = lax.axis_size("sp")
    sp_place = lax.axis_index("sp")
    seq_count = lax.axis_size("seq")
    s = lax.axis_index("seq")
    chips = seq_count // 2
    chip = s // 2
    other = s ^ 1
    listed = sources[0]

    query_parts = [lax.dynamic_slice_in_dim(queries, sp_place * head_width, head_width, 1)]
    for d in range(1, sp_count):
        columns = ((sp_place + d) % sp_count) * head_width
        piece = lax.dynamic_slice_in_dim(queries, columns, head_width, 1)
        query_parts.append(
            lax.ppermute(piece, "sp", [(i, (i + d) % sp_count) for i in range(sp_count)])
        )
    query_block = jnp.concatenate(query_parts, axis=0)

    back = [(i, (i - 2) % seq_count) for i in range(seq_count)]
    forth = [(i, (i + 2) % seq_count) for i in range(seq_count)]
    t = (s - 2) % seq_count
    t_chip = t // 2
    remote_ids = [seq_count + t, seq_count + (t ^ 1), t, t ^ 1]
    remote_valid = [
        s >= 2,
        s >= 2,
        (t_chip == 0) | (t_chip == chips - 1),
        (t_chip == 0) | (t_chip == chips - 1),
    ]
    if chips > 2:
        remote_ids += [t % 2, 1 - t % 2]
        remote_valid += [(t_chip >= 1) & (t_chip <= chips - 2)] * 2
    remote_flags = membership(listed, remote_ids, remote_valid)
    got_query, got_flags = lax.ppermute((query_block, remote_flags), "seq", back)

    swap = [(i, i ^ 1) for i in range(seq_count)]
    partner_k, partner_v, partner_ck, partner_cv = lax.ppermute(
        (new_keys, new_values, cache_keys, cache_values), "seq", swap
    )
    keys = [new_keys, partner_k, cache_keys, partner_ck]
    values = [new_values, partner_v, cache_values, partner_cv]

    if chips > 2:
        first = (cache_keys, cache_values)
        span = 1
        while span < chips - 1:
            pairs = [
                (2 * c + k, 2 * (c + span) + k)
                for c in range(span)
                if c + span < chips - 1
                for k in range(2)
            ]
            got = lax.ppermute(first, "seq", pairs)
            taking = (chip >= span) & (chip < 2 * span)
            first = tuple(jnp.where(taking, b, a) for a, b in zip(first, got))
            span *= 2
        first_other = lax.ppermute(first, "seq", swap)
        remote_keys = keys + [first[0], first_other[0]]
        remote_values = values + [first[1], first_other[1]]
    else:
        remote_keys, remote_values = keys, values

    local_flags = membership(
        listed,
        [seq_count + s, seq_count + other, s, other],
        [s >= 0, s >= 0, chip == 0, chip == 0],
    )
    local_out, local_lse = attend_partial(local_flags, query_block, keys, values, jnp.float32)

    far_out, far_lse = attend_partial(got_flags, got_query, remote_keys, remote_values, jnp.bfloat16)
    far_out, far_lse = lax.ppermute((far_out, far_lse), "seq", forth)

    rows_all = query_block.shape[0]
    lse_a = local_lse[:, 0, :][:, :, None]
    lse_b = far_lse[:, 0, :][:, :, None]
    top = jnp.maximum(lse_a, lse_b)
    weight_a = jnp.exp(lse_a - top)
    weight_b = jnp.exp(lse_b - top)
    mixed = (local_out * weight_a + far_out.astype(jnp.float32) * weight_b) / (weight_a + weight_b)
    heads_out = jnp.transpose(mixed.astype(jnp.bfloat16), (1, 0, 2)).reshape(rows_all, head_width)

    rows = queries.shape[0]
    result = jnp.zeros((rows, queries.shape[1]), jnp.bfloat16)
    for d in range(sp_count):
        piece = heads_out[d * rows : (d + 1) * rows]
        if d:
            piece = lax.ppermute(piece, "sp", [(i, (i - d) % sp_count) for i in range(sp_count)])
        columns = ((sp_place + d) % sp_count) * head_width
        result = lax.dynamic_update_slice_in_dim(result, piece, columns, 1)
    return result


def solution(mesh):
    return jax.shard_map(
        local,
        mesh=mesh,
        in_specs=(
            P(("groups", "seq", "sp"), None),
            P(("groups", "seq"), "sp"),
            P(("groups", "seq"), "sp"),
            P(("groups", "seq"), "sp"),
            P(("groups", "seq"), "sp"),
            P(("groups", "seq"), None),
        ),
        out_specs=P(("groups", "seq", "sp"), None),
        check_vma=False,
    )
```

```python
import math

import jax
import jax.numpy as jnp
from jax import lax
from jax.experimental import pallas as pl
from jax.experimental.pallas import tpu as pltpu
from jax.sharding import PartitionSpec as P

HEAD_DIM = 128
ROW_SPLIT = 2
STAT_ROWS = 8


def partial_kernel(nsrc, flags_ref, q_ref, *refs):
    key_refs = refs[:nsrc]
    value_refs = refs[nsrc : 2 * nsrc]
    out_ref, lse_ref = refs[2 * nsrc : 2 * nsrc + 2]
    score_ref = refs[2 * nsrc + 2]
    score_scale = 1.0 / math.sqrt(HEAD_DIM)
    query = q_ref[...]
    top = None
    for j in range(nsrc):
        scores = lax.dot_general(
            query, key_refs[j][...], (((1,), (1,)), ((), ())), preferred_element_type=jnp.float32
        ) * score_scale
        scores = jnp.where(flags_ref[j] > 0, scores, -1e30)
        score_ref[j] = scores
        block_top = jnp.max(scores, axis=1, keepdims=True)
        top = block_top if top is None else jnp.maximum(top, block_top)
    total = None
    summed = None
    for j in range(nsrc):
        weights = jnp.exp(score_ref[j] - top)
        part_total = jnp.sum(weights, axis=1, keepdims=True)
        product = jnp.dot(
            weights.astype(jnp.bfloat16), value_refs[j][...], preferred_element_type=jnp.float32
        )
        total = part_total if total is None else total + part_total
        summed = product if summed is None else summed + product
    out_ref[...] = (summed / total).astype(out_ref.dtype)
    lse = top + jnp.log(total)
    wide = jnp.broadcast_to(lse, (lse.shape[0], 128))
    lse_ref[...] = jnp.transpose(wide)[:STAT_ROWS]


def attend_partial(flags, query_block, key_blocks, value_blocks, out_dtype):
    nsrc = len(key_blocks)
    rows, width = query_block.shape
    block_rows = key_blocks[0].shape[0]
    nheads = width // HEAD_DIM
    row_tile = rows // ROW_SPLIT
    q_spec = pl.BlockSpec((row_tile, HEAD_DIM), lambda h, r, f: (r, h))
    kv_spec = pl.BlockSpec((block_rows, HEAD_DIM), lambda h, r, f: (0, h))
    out_spec = pl.BlockSpec((None, row_tile, HEAD_DIM), lambda h, r, f: (h, r, 0))
    lse_spec = pl.BlockSpec((None, STAT_ROWS, row_tile), lambda h, r, f: (h, 0, r))
    grid_spec = pltpu.PrefetchScalarGridSpec(
        num_scalar_prefetch=1,
        grid=(nheads, ROW_SPLIT),
        in_specs=[q_spec] + [kv_spec] * (2 * nsrc),
        out_specs=[out_spec, lse_spec],
        scratch_shapes=[pltpu.VMEM((nsrc, row_tile, block_rows), jnp.float32)],
    )
    return pl.pallas_call(
        lambda *a: partial_kernel(nsrc, *a),
        grid_spec=grid_spec,
        out_shape=[
            jax.ShapeDtypeStruct((nheads, rows, HEAD_DIM), out_dtype),
            jax.ShapeDtypeStruct((nheads, STAT_ROWS, rows), jnp.float32),
        ],
        compiler_params=pltpu.CompilerParams(dimension_semantics=("parallel", "arbitrary")),
    )(flags, query_block, *key_blocks, *value_blocks)


def membership(listed, block_ids, valid):
    hit = jnp.any(listed[None, :] == jnp.stack(block_ids)[:, None], axis=1)
    return (hit & jnp.stack(valid)).astype(jnp.int32)


def local(queries, new_keys, new_values, cache_keys, cache_values, sources):
    head_width = new_keys.shape[1]
    nheads = head_width // HEAD_DIM
    sp_count = lax.axis_size("sp")
    sp_place = lax.axis_index("sp")
    seq_count = lax.axis_size("seq")
    s = lax.axis_index("seq")
    chips = seq_count // 2
    chip = s // 2
    other = s ^ 1
    listed = sources[0]

    query_parts = [lax.dynamic_slice_in_dim(queries, sp_place * head_width, head_width, 1)]
    for d in range(1, sp_count):
        columns = ((sp_place + d) % sp_count) * head_width
        piece = lax.dynamic_slice_in_dim(queries, columns, head_width, 1)
        query_parts.append(
            lax.ppermute(piece, "sp", [(i, (i + d) % sp_count) for i in range(sp_count)])
        )
    query_block = jnp.concatenate(query_parts, axis=0)

    back = [(i, (i - 2) % seq_count) for i in range(seq_count)]
    forth = [(i, (i + 2) % seq_count) for i in range(seq_count)]
    t = (s - 2) % seq_count
    t_chip = t // 2
    remote_ids = [seq_count + t, seq_count + (t ^ 1), t, t ^ 1]
    remote_valid = [
        s >= 2,
        s >= 2,
        (t_chip == 0) | (t_chip == chips - 1),
        (t_chip == 0) | (t_chip == chips - 1),
    ]
    if chips > 2:
        remote_ids += [t % 2, 1 - t % 2]
        remote_valid += [(t_chip >= 1) & (t_chip <= chips - 2)] * 2
    remote_flags = membership(listed, remote_ids, remote_valid)
    got_query, got_flags = lax.ppermute((query_block, remote_flags), "seq", back)

    swap = [(i, i ^ 1) for i in range(seq_count)]
    partner_k, partner_v, partner_ck, partner_cv = lax.ppermute(
        (new_keys, new_values, cache_keys, cache_values), "seq", swap
    )
    keys = [new_keys, partner_k, cache_keys, partner_ck]
    values = [new_values, partner_v, cache_values, partner_cv]

    if chips > 2:
        first = (cache_keys, cache_values)
        span = 1
        while span < chips - 1:
            pairs = [
                (2 * c + k, 2 * (c + span) + k)
                for c in range(span)
                if c + span < chips - 1
                for k in range(2)
            ]
            got = lax.ppermute(first, "seq", pairs)
            taking = (chip >= span) & (chip < 2 * span)
            first = tuple(jnp.where(taking, b, a) for a, b in zip(first, got))
            span *= 2
        first_other = lax.ppermute(first, "seq", swap)
        remote_keys = keys + [first[0], first_other[0]]
        remote_values = values + [first[1], first_other[1]]
    else:
        remote_keys, remote_values = keys, values

    local_flags = membership(
        listed,
        [seq_count + s, seq_count + other, s, other],
        [s >= 0, s >= 0, chip == 0, chip == 0],
    )
    local_out, local_lse = attend_partial(local_flags, query_block, keys, values, jnp.float32)

    far_out, far_lse = attend_partial(got_flags, got_query, remote_keys, remote_values, jnp.bfloat16)
    far_out, far_lse = lax.ppermute((far_out, far_lse), "seq", forth)

    rows_all = query_block.shape[0]
    lse_a = local_lse[:, 0, :][:, :, None]
    lse_b = far_lse[:, 0, :][:, :, None]
    top = jnp.maximum(lse_a, lse_b)
    weight_a = jnp.exp(lse_a - top)
    weight_b = jnp.exp(lse_b - top)
    mixed = (local_out * weight_a + far_out.astype(jnp.float32) * weight_b) / (weight_a + weight_b)
    heads_out = jnp.transpose(mixed.astype(jnp.bfloat16), (1, 0, 2)).reshape(rows_all, head_width)

    rows = queries.shape[0]
    result = jnp.zeros((rows, queries.shape[1]), jnp.bfloat16)
    for d in range(sp_count):
        piece = heads_out[d * rows : (d + 1) * rows]
        if d:
            piece = lax.ppermute(piece, "sp", [(i, (i - d) % sp_count) for i in range(sp_count)])
        columns = ((sp_place + d) % sp_count) * head_width
        result = lax.dynamic_update_slice_in_dim(result, piece, columns, 1)
    return result


def solution(mesh):
    return jax.shard_map(
        local,
        mesh=mesh,
        in_specs=(
            P(("groups", "seq", "sp"), None),
            P(("groups", "seq"), "sp"),
            P(("groups", "seq"), "sp"),
            P(("groups", "seq"), "sp"),
            P(("groups", "seq"), "sp"),
            P(("groups", "seq"), None),
        ),
        out_specs=P(("groups", "seq", "sp"), None),
        check_vma=False,
    )
```

```python
import math

import jax
import jax.numpy as jnp
from jax import lax
from jax.experimental import pallas as pl
from jax.experimental.pallas import tpu as pltpu
from jax.sharding import PartitionSpec as P

HEAD_DIM = 128
ROW_SPLIT = 2
STAT_ROWS = 8


def partial_kernel(nsrc, flags_ref, q_ref, *refs):
    key_refs = refs[:nsrc]
    value_refs = refs[nsrc : 2 * nsrc]
    out_ref, lse_ref = refs[2 * nsrc : 2 * nsrc + 2]
    score_ref = refs[2 * nsrc + 2]
    score_scale = 1.0 / math.sqrt(HEAD_DIM)
    query = q_ref[...]
    top = None
    for j in range(nsrc):
        raw = lax.dot_general(
            query, key_refs[j][...], (((1,), (1,)), ((), ())), preferred_element_type=jnp.float32
        )
        score_ref[j] = raw
        block_top = jnp.where(flags_ref[j] > 0, jnp.max(raw, axis=1, keepdims=True), -1e30)
        top = block_top if top is None else jnp.maximum(top, block_top)
    top = top * score_scale
    ones = jnp.ones((score_ref.shape[2], HEAD_DIM), jnp.bfloat16)
    total = None
    summed = None
    for j in range(nsrc):
        shift = jnp.where(flags_ref[j] > 0, top, 1e30)
        weights = jnp.exp(score_ref[j] * score_scale - shift).astype(jnp.bfloat16)
        part_total = jnp.dot(weights, ones, preferred_element_type=jnp.float32)
        product = jnp.dot(weights, value_refs[j][...], preferred_element_type=jnp.float32)
        total = part_total if total is None else total + part_total
        summed = product if summed is None else summed + product
    filled = total > 0
    safe = jnp.where(filled, total, 1.0)
    out_ref[...] = (summed / safe).astype(out_ref.dtype)
    lse = jnp.where(filled, top + jnp.log(safe), -1e30)
    lse_ref[...] = jnp.transpose(lse)[:STAT_ROWS]


def attend_partial(flags, query_block, key_blocks, value_blocks, out_dtype):
    nsrc = len(key_blocks)
    rows, width = query_block.shape
    block_rows = key_blocks[0].shape[0]
    nheads = width // HEAD_DIM
    row_tile = rows // ROW_SPLIT
    q_spec = pl.BlockSpec((row_tile, HEAD_DIM), lambda h, r, f: (r, h))
    kv_spec = pl.BlockSpec((block_rows, HEAD_DIM), lambda h, r, f: (0, h))
    out_spec = pl.BlockSpec((None, row_tile, HEAD_DIM), lambda h, r, f: (h, r, 0))
    lse_spec = pl.BlockSpec((None, STAT_ROWS, row_tile), lambda h, r, f: (h, 0, r))
    grid_spec = pltpu.PrefetchScalarGridSpec(
        num_scalar_prefetch=1,
        grid=(nheads, ROW_SPLIT),
        in_specs=[q_spec] + [kv_spec] * (2 * nsrc),
        out_specs=[out_spec, lse_spec],
        scratch_shapes=[pltpu.VMEM((nsrc, row_tile, block_rows), jnp.float32)],
    )
    return pl.pallas_call(
        lambda *a: partial_kernel(nsrc, *a),
        grid_spec=grid_spec,
        out_shape=[
            jax.ShapeDtypeStruct((nheads, rows, HEAD_DIM), out_dtype),
            jax.ShapeDtypeStruct((nheads, STAT_ROWS, rows), jnp.float32),
        ],
        compiler_params=pltpu.CompilerParams(dimension_semantics=("parallel", "arbitrary")),
    )(flags, query_block, *key_blocks, *value_blocks)


def membership(listed, block_ids, valid):
    hit = jnp.any(listed[None, :] == jnp.stack(block_ids)[:, None], axis=1)
    return (hit & jnp.stack(valid)).astype(jnp.int32)


def local(queries, new_keys, new_values, cache_keys, cache_values, sources):
    head_width = new_keys.shape[1]
    nheads = head_width // HEAD_DIM
    sp_count = lax.axis_size("sp")
    sp_place = lax.axis_index("sp")
    seq_count = lax.axis_size("seq")
    s = lax.axis_index("seq")
    chips = seq_count // 2
    chip = s // 2
    other = s ^ 1
    listed = sources[0]

    query_parts = [lax.dynamic_slice_in_dim(queries, sp_place * head_width, head_width, 1)]
    for d in range(1, sp_count):
        columns = ((sp_place + d) % sp_count) * head_width
        piece = lax.dynamic_slice_in_dim(queries, columns, head_width, 1)
        query_parts.append(
            lax.ppermute(piece, "sp", [(i, (i + d) % sp_count) for i in range(sp_count)])
        )
    query_block = jnp.concatenate(query_parts, axis=0)

    back = [(i, (i - 2) % seq_count) for i in range(seq_count)]
    forth = [(i, (i + 2) % seq_count) for i in range(seq_count)]
    t = (s - 2) % seq_count
    t_chip = t // 2
    remote_ids = [seq_count + t, seq_count + (t ^ 1), t, t ^ 1]
    remote_valid = [
        s >= 2,
        s >= 2,
        (t_chip == 0) | (t_chip == chips - 1),
        (t_chip == 0) | (t_chip == chips - 1),
    ]
    if chips > 2:
        remote_ids += [t % 2, 1 - t % 2]
        remote_valid += [(t_chip >= 1) & (t_chip <= chips - 2)] * 2
    remote_flags = membership(listed, remote_ids, remote_valid)
    got_query, got_flags = lax.ppermute((query_block, remote_flags), "seq", back)

    swap = [(i, i ^ 1) for i in range(seq_count)]
    partner_k, partner_v, partner_ck, partner_cv = lax.ppermute(
        (new_keys, new_values, cache_keys, cache_values), "seq", swap
    )
    keys = [new_keys, partner_k, cache_keys, partner_ck]
    values = [new_values, partner_v, cache_values, partner_cv]

    if chips > 2:
        first = (cache_keys, cache_values)
        span = 1
        while span < chips - 1:
            pairs = [
                (2 * c + k, 2 * (c + span) + k)
                for c in range(span)
                if c + span < chips - 1
                for k in range(2)
            ]
            got = lax.ppermute(first, "seq", pairs)
            taking = (chip >= span) & (chip < 2 * span)
            first = tuple(jnp.where(taking, b, a) for a, b in zip(first, got))
            span *= 2
        first_other = lax.ppermute(first, "seq", swap)
        remote_keys = keys + [first[0], first_other[0]]
        remote_values = values + [first[1], first_other[1]]
    else:
        remote_keys, remote_values = keys, values

    local_flags = membership(
        listed,
        [seq_count + s, seq_count + other, s, other],
        [s >= 0, s >= 0, chip == 0, chip == 0],
    )
    local_out, local_lse = attend_partial(local_flags, query_block, keys, values, jnp.float32)

    far_out, far_lse = attend_partial(got_flags, got_query, remote_keys, remote_values, jnp.bfloat16)
    far_out, far_lse = lax.ppermute((far_out, far_lse), "seq", forth)

    rows_all = query_block.shape[0]
    lse_a = local_lse[:, 0, :][:, :, None]
    lse_b = far_lse[:, 0, :][:, :, None]
    top = jnp.maximum(lse_a, lse_b)
    weight_a = jnp.exp(lse_a - top)
    weight_b = jnp.exp(lse_b - top)
    mixed = (local_out * weight_a + far_out.astype(jnp.float32) * weight_b) / (weight_a + weight_b)
    heads_out = jnp.transpose(mixed.astype(jnp.bfloat16), (1, 0, 2)).reshape(rows_all, head_width)

    rows = queries.shape[0]
    result = jnp.zeros((rows, queries.shape[1]), jnp.bfloat16)
    for d in range(sp_count):
        piece = heads_out[d * rows : (d + 1) * rows]
        if d:
            piece = lax.ppermute(piece, "sp", [(i, (i - d) % sp_count) for i in range(sp_count)])
        columns = ((sp_place + d) % sp_count) * head_width
        result = lax.dynamic_update_slice_in_dim(result, piece, columns, 1)
    return result


def solution(mesh):
    return jax.shard_map(
        local,
        mesh=mesh,
        in_specs=(
            P(("groups", "seq", "sp"), None),
            P(("groups", "seq"), "sp"),
            P(("groups", "seq"), "sp"),
            P(("groups", "seq"), "sp"),
            P(("groups", "seq"), "sp"),
            P(("groups", "seq"), None),
        ),
        out_specs=P(("groups", "seq", "sp"), None),
        check_vma=False,
    )
```

```python
import math

import jax
import jax.numpy as jnp
from jax import lax
from jax.experimental import pallas as pl
from jax.experimental.pallas import tpu as pltpu
from jax.sharding import PartitionSpec as P

HEAD_DIM = 128
ROW_SPLIT = 2
STAT_ROWS = 8


def partial_kernel(nsrc, flags_ref, q_ref, *refs):
    key_refs = refs[:nsrc]
    value_refs = refs[nsrc : 2 * nsrc]
    out_ref, lse_ref = refs[2 * nsrc : 2 * nsrc + 2]
    score_ref = refs[2 * nsrc + 2]
    score_scale = 1.0 / math.sqrt(HEAD_DIM)
    query = q_ref[...]
    top = None
    for j in range(nsrc):
        scores = lax.dot_general(
            query, key_refs[j][...], (((1,), (1,)), ((), ())), preferred_element_type=jnp.float32
        ) * score_scale
        scores = jnp.where(flags_ref[j] > 0, scores, -1e30)
        score_ref[j] = scores
        block_top = jnp.max(scores, axis=1, keepdims=True)
        top = block_top if top is None else jnp.maximum(top, block_top)
    total = None
    summed = None
    for j in range(nsrc):
        weights = jnp.exp(score_ref[j] - top)
        part_total = jnp.sum(weights, axis=1, keepdims=True)
        product = jnp.dot(
            weights.astype(jnp.bfloat16), value_refs[j][...], preferred_element_type=jnp.float32
        )
        total = part_total if total is None else total + part_total
        summed = product if summed is None else summed + product
    out_ref[...] = (summed / total).astype(out_ref.dtype)
    lse = top + jnp.log(total)
    wide = jnp.broadcast_to(lse, (lse.shape[0], 128))
    lse_ref[...] = jnp.transpose(wide)[:STAT_ROWS]


def attend_partial(flags, query_block, key_blocks, value_blocks, out_dtype):
    nsrc = len(key_blocks)
    rows, width = query_block.shape
    block_rows = key_blocks[0].shape[0]
    nheads = width // HEAD_DIM
    row_tile = rows // ROW_SPLIT
    q_spec = pl.BlockSpec((row_tile, HEAD_DIM), lambda h, r, f: (r, h))
    kv_spec = pl.BlockSpec((block_rows, HEAD_DIM), lambda h, r, f: (0, h))
    out_spec = pl.BlockSpec((None, row_tile, HEAD_DIM), lambda h, r, f: (h, r, 0))
    lse_spec = pl.BlockSpec((None, STAT_ROWS, row_tile), lambda h, r, f: (h, 0, r))
    grid_spec = pltpu.PrefetchScalarGridSpec(
        num_scalar_prefetch=1,
        grid=(nheads, ROW_SPLIT),
        in_specs=[q_spec] + [kv_spec] * (2 * nsrc),
        out_specs=[out_spec, lse_spec],
        scratch_shapes=[pltpu.VMEM((nsrc, row_tile, block_rows), jnp.float32)],
    )
    return pl.pallas_call(
        lambda *a: partial_kernel(nsrc, *a),
        grid_spec=grid_spec,
        out_shape=[
            jax.ShapeDtypeStruct((nheads, rows, HEAD_DIM), out_dtype),
            jax.ShapeDtypeStruct((nheads, STAT_ROWS, rows), jnp.float32),
        ],
        compiler_params=pltpu.CompilerParams(dimension_semantics=("parallel", "arbitrary")),
    )(flags, query_block, *key_blocks, *value_blocks)


def membership(listed, block_ids, valid):
    hit = jnp.any(listed[None, :] == jnp.stack(block_ids)[:, None], axis=1)
    return (hit & jnp.stack(valid)).astype(jnp.int32)


def local(queries, new_keys, new_values, cache_keys, cache_values, sources):
    head_width = new_keys.shape[1]
    nheads = head_width // HEAD_DIM
    sp_count = lax.axis_size("sp")
    sp_place = lax.axis_index("sp")
    seq_count = lax.axis_size("seq")
    s = lax.axis_index("seq")
    chips = seq_count // 2
    chip = s // 2
    other = s ^ 1
    listed = sources[0]

    query_parts = [lax.dynamic_slice_in_dim(queries, sp_place * head_width, head_width, 1)]
    for d in range(1, sp_count):
        columns = ((sp_place + d) % sp_count) * head_width
        piece = lax.dynamic_slice_in_dim(queries, columns, head_width, 1)
        query_parts.append(
            lax.ppermute(piece, "sp", [(i, (i + d) % sp_count) for i in range(sp_count)])
        )
    query_block = jnp.concatenate(query_parts, axis=0)

    back = [(i, (i - 2) % seq_count) for i in range(seq_count)]
    t = (s - 2) % seq_count
    t_chip = t // 2
    remote_ids = [seq_count + t, seq_count + (t ^ 1), t, t ^ 1]
    remote_valid = [
        s >= 2,
        s >= 2,
        (t_chip == 0) | (t_chip == chips - 1),
        (t_chip == 0) | (t_chip == chips - 1),
    ]
    if chips > 2:
        remote_ids += [t % 2, 1 - t % 2]
        remote_valid += [(t_chip >= 1) & (t_chip <= chips - 2)] * 2
    remote_flags = membership(listed, remote_ids, remote_valid)
    got_query, got_flags = lax.ppermute((query_block, remote_flags), "seq", back)

    swap = [(i, i ^ 1) for i in range(seq_count)]
    partner_k, partner_v, partner_ck, partner_cv = lax.ppermute(
        (new_keys, new_values, cache_keys, cache_values), "seq", swap
    )
    keys = [new_keys, partner_k, cache_keys, partner_ck]
    values = [new_values, partner_v, cache_values, partner_cv]

    if chips > 2:
        first = (cache_keys, cache_values)
        span = 1
        while span < chips - 1:
            pairs = [
                (2 * c + k, 2 * (c + span) + k)
                for c in range(span)
                if c + span < chips - 1
                for k in range(2)
            ]
            got = lax.ppermute(first, "seq", pairs)
            taking = (chip >= span) & (chip < 2 * span)
            first = tuple(jnp.where(taking, b, a) for a, b in zip(first, got))
            span *= 2
        first_other = lax.ppermute(first, "seq", swap)
        remote_keys = keys + [first[0], first_other[0]]
        remote_values = values + [first[1], first_other[1]]
    else:
        remote_keys, remote_values = keys, values

    local_flags = membership(
        listed,
        [seq_count + s, seq_count + other, s, other],
        [s >= 0, s >= 0, chip == 0, chip == 0],
    )
    local_out, local_lse = attend_partial(local_flags, query_block, keys, values, jnp.float32)
    got_query, local_out, local_lse = lax.optimization_barrier((got_query, local_out, local_lse))

    far_out, far_lse = attend_partial(got_flags, got_query, remote_keys, remote_values, jnp.bfloat16)
    rows = queries.shape[0]
    near_lse = local_lse[:, 0, :]
    far_lse = far_lse[:, 0, :]
    result = jnp.zeros((rows, queries.shape[1]), jnp.bfloat16)
    for d in range(sp_count):
        near_part = local_out[:, d * rows : (d + 1) * rows]
        near_stat = near_lse[:, d * rows : (d + 1) * rows]
        if d:
            near_part, near_stat = lax.ppermute(
                (near_part.astype(jnp.bfloat16), near_stat),
                "sp",
                [(i, (i - d) % sp_count) for i in range(sp_count)],
            )
        diagonal = [
            (i * sp_count + j, ((i + 2) % seq_count) * sp_count + (j - d) % sp_count)
            for i in range(seq_count)
            for j in range(sp_count)
        ]
        far_part, far_stat = lax.ppermute(
            (far_out[:, d * rows : (d + 1) * rows], far_lse[:, d * rows : (d + 1) * rows]),
            ("seq", "sp"),
            diagonal,
        )
        lse_a = near_stat[:, :, None]
        lse_b = far_stat[:, :, None]
        top = jnp.maximum(lse_a, lse_b)
        weight_a = jnp.exp(lse_a - top)
        weight_b = jnp.exp(lse_b - top)
        mixed = (
            near_part.astype(jnp.float32) * weight_a + far_part.astype(jnp.float32) * weight_b
        ) / (weight_a + weight_b)
        piece = jnp.transpose(mixed.astype(jnp.bfloat16), (1, 0, 2)).reshape(rows, head_width)
        columns = ((sp_place + d) % sp_count) * head_width
        result = lax.dynamic_update_slice_in_dim(result, piece, columns, 1)
    return result


def solution(mesh):
    return jax.shard_map(
        local,
        mesh=mesh,
        in_specs=(
            P(("groups", "seq", "sp"), None),
            P(("groups", "seq"), "sp"),
            P(("groups", "seq"), "sp"),
            P(("groups", "seq"), "sp"),
            P(("groups", "seq"), "sp"),
            P(("groups", "seq"), None),
        ),
        out_specs=P(("groups", "seq", "sp"), None),
        check_vma=False,
    )
```

```python
import math

import jax
import jax.numpy as jnp
from jax import lax
from jax.experimental import pallas as pl
from jax.experimental.pallas import tpu as pltpu
from jax.sharding import PartitionSpec as P

HEAD_DIM = 128
ROW_SPLIT = 2
STAT_ROWS = 8


def partial_kernel(nsrc, group, flags_ref, q_ref, *refs):
    key_refs = refs[:nsrc]
    value_refs = refs[nsrc : 2 * nsrc]
    out_ref, lse_ref = refs[2 * nsrc : 2 * nsrc + 2]
    score_ref = refs[2 * nsrc + 2]
    score_scale = 1.0 / math.sqrt(HEAD_DIM)
    for g in range(group):
        cols = slice(g * HEAD_DIM, (g + 1) * HEAD_DIM)
        query = q_ref[:, cols]
        top = None
        for j in range(nsrc):
            scores = lax.dot_general(
                query,
                key_refs[j][:, cols],
                (((1,), (1,)), ((), ())),
                preferred_element_type=jnp.float32,
            ) * score_scale
            scores = jnp.where(flags_ref[j] > 0, scores, -1e30)
            score_ref[j] = scores
            block_top = jnp.max(scores, axis=1, keepdims=True)
            top = block_top if top is None else jnp.maximum(top, block_top)
        total = None
        summed = None
        for j in range(nsrc):
            weights = jnp.exp(score_ref[j] - top)
            part_total = jnp.sum(weights, axis=1, keepdims=True)
            product = jnp.dot(
                weights.astype(jnp.bfloat16), value_refs[j][:, cols], preferred_element_type=jnp.float32
            )
            total = part_total if total is None else total + part_total
            summed = product if summed is None else summed + product
        out_ref[g] = (summed / total).astype(out_ref.dtype)
        lse = top + jnp.log(total)
        wide = jnp.broadcast_to(lse, (lse.shape[0], 128))
        lse_ref[g] = jnp.transpose(wide)[:STAT_ROWS]


def attend_partial(flags, query_block, key_blocks, value_blocks, out_dtype):
    nsrc = len(key_blocks)
    rows, width = query_block.shape
    block_rows = key_blocks[0].shape[0]
    nheads = width // HEAD_DIM
    group = 2 if nheads % 2 == 0 else 1
    row_tile = rows // ROW_SPLIT
    span = group * HEAD_DIM
    q_spec = pl.BlockSpec((row_tile, span), lambda h, r, f: (r, h))
    kv_spec = pl.BlockSpec((block_rows, span), lambda h, r, f: (0, h))
    out_spec = pl.BlockSpec((group, row_tile, HEAD_DIM), lambda h, r, f: (h, r, 0))
    lse_spec = pl.BlockSpec((group, STAT_ROWS, row_tile), lambda h, r, f: (h, 0, r))
    grid_spec = pltpu.PrefetchScalarGridSpec(
        num_scalar_prefetch=1,
        grid=(nheads // group, ROW_SPLIT),
        in_specs=[q_spec] + [kv_spec] * (2 * nsrc),
        out_specs=[out_spec, lse_spec],
        scratch_shapes=[pltpu.VMEM((nsrc, row_tile, block_rows), jnp.float32)],
    )
    return pl.pallas_call(
        lambda *a: partial_kernel(nsrc, group, *a),
        grid_spec=grid_spec,
        out_shape=[
            jax.ShapeDtypeStruct((nheads, rows, HEAD_DIM), out_dtype),
            jax.ShapeDtypeStruct((nheads, STAT_ROWS, rows), jnp.float32),
        ],
        compiler_params=pltpu.CompilerParams(dimension_semantics=("parallel", "arbitrary")),
    )(flags, query_block, *key_blocks, *value_blocks)


def membership(listed, block_ids, valid):
    hit = jnp.any(listed[None, :] == jnp.stack(block_ids)[:, None], axis=1)
    return (hit & jnp.stack(valid)).astype(jnp.int32)


def local(queries, new_keys, new_values, cache_keys, cache_values, sources):
    head_width = new_keys.shape[1]
    nheads = head_width // HEAD_DIM
    sp_count = lax.axis_size("sp")
    sp_place = lax.axis_index("sp")
    seq_count = lax.axis_size("seq")
    s = lax.axis_index("seq")
    chips = seq_count // 2
    chip = s // 2
    other = s ^ 1
    listed = sources[0]

    query_parts = [lax.dynamic_slice_in_dim(queries, sp_place * head_width, head_width, 1)]
    for d in range(1, sp_count):
        columns = ((sp_place + d) % sp_count) * head_width
        piece = lax.dynamic_slice_in_dim(queries, columns, head_width, 1)
        query_parts.append(
            lax.ppermute(piece, "sp", [(i, (i + d) % sp_count) for i in range(sp_count)])
        )
    query_block = jnp.concatenate(query_parts, axis=0)

    back = [(i, (i - 2) % seq_count) for i in range(seq_count)]
    forth = [(i, (i + 2) % seq_count) for i in range(seq_count)]
    t = (s - 2) % seq_count
    t_chip = t // 2
    remote_ids = [seq_count + t, seq_count + (t ^ 1), t, t ^ 1]
    remote_valid = [
        s >= 2,
        s >= 2,
        (t_chip == 0) | (t_chip == chips - 1),
        (t_chip == 0) | (t_chip == chips - 1),
    ]
    if chips > 2:
        remote_ids += [t % 2, 1 - t % 2]
        remote_valid += [(t_chip >= 1) & (t_chip <= chips - 2)] * 2
    remote_flags = membership(listed, remote_ids, remote_valid)
    got_query, got_flags = lax.ppermute((query_block, remote_flags), "seq", back)

    swap = [(i, i ^ 1) for i in range(seq_count)]
    partner_k, partner_v, partner_ck, partner_cv = lax.ppermute(
        (new_keys, new_values, cache_keys, cache_values), "seq", swap
    )
    keys = [new_keys, partner_k, cache_keys, partner_ck]
    values = [new_values, partner_v, cache_values, partner_cv]

    if chips > 2:
        first = (cache_keys, cache_values)
        span = 1
        while span < chips - 1:
            pairs = [
                (2 * c + k, 2 * (c + span) + k)
                for c in range(span)
                if c + span < chips - 1
                for k in range(2)
            ]
            got = lax.ppermute(first, "seq", pairs)
            taking = (chip >= span) & (chip < 2 * span)
            first = tuple(jnp.where(taking, b, a) for a, b in zip(first, got))
            span *= 2
        first_other = lax.ppermute(first, "seq", swap)
        remote_keys = keys + [first[0], first_other[0]]
        remote_values = values + [first[1], first_other[1]]
    else:
        remote_keys, remote_values = keys, values

    local_flags = membership(
        listed,
        [seq_count + s, seq_count + other, s, other],
        [s >= 0, s >= 0, chip == 0, chip == 0],
    )
    local_out, local_lse = attend_partial(local_flags, query_block, keys, values, jnp.float32)

    far_out, far_lse = attend_partial(got_flags, got_query, remote_keys, remote_values, jnp.bfloat16)
    far_out, far_lse = lax.ppermute((far_out, far_lse), "seq", forth)

    rows_all = query_block.shape[0]
    lse_a = local_lse[:, 0, :][:, :, None]
    lse_b = far_lse[:, 0, :][:, :, None]
    top = jnp.maximum(lse_a, lse_b)
    weight_a = jnp.exp(lse_a - top)
    weight_b = jnp.exp(lse_b - top)
    mixed = (local_out * weight_a + far_out.astype(jnp.float32) * weight_b) / (weight_a + weight_b)
    heads_out = jnp.transpose(mixed.astype(jnp.bfloat16), (1, 0, 2)).reshape(rows_all, head_width)

    rows = queries.shape[0]
    result = jnp.zeros((rows, queries.shape[1]), jnp.bfloat16)
    for d in range(sp_count):
        piece = heads_out[d * rows : (d + 1) * rows]
        if d:
            piece = lax.ppermute(piece, "sp", [(i, (i - d) % sp_count) for i in range(sp_count)])
        columns = ((sp_place + d) % sp_count) * head_width
        result = lax.dynamic_update_slice_in_dim(result, piece, columns, 1)
    return result


def solution(mesh):
    return jax.shard_map(
        local,
        mesh=mesh,
        in_specs=(
            P(("groups", "seq", "sp"), None),
            P(("groups", "seq"), "sp"),
            P(("groups", "seq"), "sp"),
            P(("groups", "seq"), "sp"),
            P(("groups", "seq"), "sp"),
            P(("groups", "seq"), None),
        ),
        out_specs=P(("groups", "seq", "sp"), None),
        check_vma=False,
    )
```

```python
import math

import jax
import jax.numpy as jnp
from jax import lax
from jax.experimental import pallas as pl
from jax.experimental.pallas import tpu as pltpu
from jax.sharding import PartitionSpec as P

HEAD_DIM = 128
ROW_SPLIT = 2
STAT_ROWS = 8


def partial_kernel(nsrc, group, flags_ref, q_ref, *refs):
    key_refs = refs[:nsrc]
    value_refs = refs[nsrc : 2 * nsrc]
    out_ref, lse_ref = refs[2 * nsrc : 2 * nsrc + 2]
    score_ref = refs[2 * nsrc + 2]
    score_scale = 1.0 / math.sqrt(HEAD_DIM)
    for g in range(group):
        cols = slice(g * HEAD_DIM, (g + 1) * HEAD_DIM)
        query = q_ref[:, cols]
        top = None
        for j in range(nsrc):
            scores = lax.dot_general(
                query,
                key_refs[j][:, cols],
                (((1,), (1,)), ((), ())),
                preferred_element_type=jnp.float32,
            ) * score_scale
            scores = jnp.where(flags_ref[j] > 0, scores, -1e30)
            score_ref[j] = scores
            block_top = jnp.max(scores, axis=1, keepdims=True)
            top = block_top if top is None else jnp.maximum(top, block_top)
        total = None
        summed = None
        for j in range(nsrc):
            weights = jnp.exp(score_ref[j] - top)
            part_total = jnp.sum(weights, axis=1, keepdims=True)
            product = jnp.dot(
                weights.astype(jnp.bfloat16), value_refs[j][:, cols], preferred_element_type=jnp.float32
            )
            total = part_total if total is None else total + part_total
            summed = product if summed is None else summed + product
        out_ref[g] = (summed / total).astype(out_ref.dtype)
        lse = top + jnp.log(total)
        wide = jnp.broadcast_to(lse, (lse.shape[0], 128))
        lse_ref[g] = jnp.transpose(wide)[:STAT_ROWS]


def attend_partial(flags, query_block, key_blocks, value_blocks, out_dtype):
    nsrc = len(key_blocks)
    rows, width = query_block.shape
    block_rows = key_blocks[0].shape[0]
    nheads = width // HEAD_DIM
    group = max(g for g in range(1, 6) if nheads % g == 0)
    row_tile = rows // ROW_SPLIT
    span = group * HEAD_DIM
    q_spec = pl.BlockSpec((row_tile, span), lambda h, r, f: (r, h))
    kv_spec = pl.BlockSpec((block_rows, span), lambda h, r, f: (0, h))
    out_spec = pl.BlockSpec((group, row_tile, HEAD_DIM), lambda h, r, f: (h, r, 0))
    lse_spec = pl.BlockSpec((group, STAT_ROWS, row_tile), lambda h, r, f: (h, 0, r))
    grid_spec = pltpu.PrefetchScalarGridSpec(
        num_scalar_prefetch=1,
        grid=(nheads // group, ROW_SPLIT),
        in_specs=[q_spec] + [kv_spec] * (2 * nsrc),
        out_specs=[out_spec, lse_spec],
        scratch_shapes=[pltpu.VMEM((nsrc, row_tile, block_rows), jnp.float32)],
    )
    return pl.pallas_call(
        lambda *a: partial_kernel(nsrc, group, *a),
        grid_spec=grid_spec,
        out_shape=[
            jax.ShapeDtypeStruct((nheads, rows, HEAD_DIM), out_dtype),
            jax.ShapeDtypeStruct((nheads, STAT_ROWS, rows), jnp.float32),
        ],
        compiler_params=pltpu.CompilerParams(dimension_semantics=("parallel", "arbitrary")),
    )(flags, query_block, *key_blocks, *value_blocks)


def membership(listed, block_ids, valid):
    hit = jnp.any(listed[None, :] == jnp.stack(block_ids)[:, None], axis=1)
    return (hit & jnp.stack(valid)).astype(jnp.int32)


def local(queries, new_keys, new_values, cache_keys, cache_values, sources):
    head_width = new_keys.shape[1]
    nheads = head_width // HEAD_DIM
    sp_count = lax.axis_size("sp")
    sp_place = lax.axis_index("sp")
    seq_count = lax.axis_size("seq")
    s = lax.axis_index("seq")
    chips = seq_count // 2
    chip = s // 2
    other = s ^ 1
    listed = sources[0]

    query_parts = [lax.dynamic_slice_in_dim(queries, sp_place * head_width, head_width, 1)]
    for d in range(1, sp_count):
        columns = ((sp_place + d) % sp_count) * head_width
        piece = lax.dynamic_slice_in_dim(queries, columns, head_width, 1)
        query_parts.append(
            lax.ppermute(piece, "sp", [(i, (i + d) % sp_count) for i in range(sp_count)])
        )
    query_block = jnp.concatenate(query_parts, axis=0)

    back = [(i, (i - 2) % seq_count) for i in range(seq_count)]
    forth = [(i, (i + 2) % seq_count) for i in range(seq_count)]
    t = (s - 2) % seq_count
    t_chip = t // 2
    remote_ids = [seq_count + t, seq_count + (t ^ 1), t, t ^ 1]
    remote_valid = [
        s >= 2,
        s >= 2,
        (t_chip == 0) | (t_chip == chips - 1),
        (t_chip == 0) | (t_chip == chips - 1),
    ]
    if chips > 2:
        remote_ids += [t % 2, 1 - t % 2]
        remote_valid += [(t_chip >= 1) & (t_chip <= chips - 2)] * 2
    remote_flags = membership(listed, remote_ids, remote_valid)
    got_query, got_flags = lax.ppermute((query_block, remote_flags), "seq", back)

    swap = [(i, i ^ 1) for i in range(seq_count)]
    partner_k, partner_v, partner_ck, partner_cv = lax.ppermute(
        (new_keys, new_values, cache_keys, cache_values), "seq", swap
    )
    keys = [new_keys, partner_k, cache_keys, partner_ck]
    values = [new_values, partner_v, cache_values, partner_cv]

    if chips > 2:
        first = (cache_keys, cache_values)
        span = 1
        while span < chips - 1:
            pairs = [
                (2 * c + k, 2 * (c + span) + k)
                for c in range(span)
                if c + span < chips - 1
                for k in range(2)
            ]
            got = lax.ppermute(first, "seq", pairs)
            taking = (chip >= span) & (chip < 2 * span)
            first = tuple(jnp.where(taking, b, a) for a, b in zip(first, got))
            span *= 2
        first_other = lax.ppermute(first, "seq", swap)
        remote_keys = keys + [first[0], first_other[0]]
        remote_values = values + [first[1], first_other[1]]
    else:
        remote_keys, remote_values = keys, values

    local_flags = membership(
        listed,
        [seq_count + s, seq_count + other, s, other],
        [s >= 0, s >= 0, chip == 0, chip == 0],
    )
    local_out, local_lse = attend_partial(local_flags, query_block, keys, values, jnp.float32)

    far_out, far_lse = attend_partial(got_flags, got_query, remote_keys, remote_values, jnp.bfloat16)
    far_out, far_lse = lax.ppermute((far_out, far_lse), "seq", forth)

    rows_all = query_block.shape[0]
    lse_a = local_lse[:, 0, :][:, :, None]
    lse_b = far_lse[:, 0, :][:, :, None]
    top = jnp.maximum(lse_a, lse_b)
    weight_a = jnp.exp(lse_a - top)
    weight_b = jnp.exp(lse_b - top)
    mixed = (local_out * weight_a + far_out.astype(jnp.float32) * weight_b) / (weight_a + weight_b)
    heads_out = jnp.transpose(mixed.astype(jnp.bfloat16), (1, 0, 2)).reshape(rows_all, head_width)

    rows = queries.shape[0]
    result = jnp.zeros((rows, queries.shape[1]), jnp.bfloat16)
    for d in range(sp_count):
        piece = heads_out[d * rows : (d + 1) * rows]
        if d:
            piece = lax.ppermute(piece, "sp", [(i, (i - d) % sp_count) for i in range(sp_count)])
        columns = ((sp_place + d) % sp_count) * head_width
        result = lax.dynamic_update_slice_in_dim(result, piece, columns, 1)
    return result


def solution(mesh):
    return jax.shard_map(
        local,
        mesh=mesh,
        in_specs=(
            P(("groups", "seq", "sp"), None),
            P(("groups", "seq"), "sp"),
            P(("groups", "seq"), "sp"),
            P(("groups", "seq"), "sp"),
            P(("groups", "seq"), "sp"),
            P(("groups", "seq"), None),
        ),
        out_specs=P(("groups", "seq", "sp"), None),
        check_vma=False,
    )
```

```python
import math

import jax
import jax.numpy as jnp
from jax import lax
from jax.experimental import pallas as pl
from jax.experimental.pallas import tpu as pltpu
from jax.sharding import PartitionSpec as P

HEAD_DIM = 128
ROW_SPLIT = 2
STAT_ROWS = 8


def partial_kernel(nsrc, group, flags_ref, q_ref, *refs):
    key_refs = refs[:nsrc]
    value_refs = refs[nsrc : 2 * nsrc]
    out_ref, lse_ref = refs[2 * nsrc : 2 * nsrc + 2]
    score_ref = refs[2 * nsrc + 2]
    score_scale = 1.0 / math.sqrt(HEAD_DIM)
    for g in range(group):
        cols = slice(g * HEAD_DIM, (g + 1) * HEAD_DIM)
        query = q_ref[:, cols]
        top = None
        for j in range(nsrc):
            scores = lax.dot_general(
                query,
                key_refs[j][:, cols],
                (((1,), (1,)), ((), ())),
                preferred_element_type=jnp.float32,
            ) * score_scale
            scores = jnp.where(flags_ref[j] > 0, scores, -1e30)
            score_ref[j] = scores
            block_top = jnp.max(scores, axis=1, keepdims=True)
            top = block_top if top is None else jnp.maximum(top, block_top)
        total = None
        summed = None
        for j in range(nsrc):
            weights = jnp.exp(score_ref[j] - top)
            part_total = jnp.sum(weights, axis=1, keepdims=True)
            product = jnp.dot(
                weights.astype(jnp.bfloat16), value_refs[j][:, cols], preferred_element_type=jnp.float32
            )
            total = part_total if total is None else total + part_total
            summed = product if summed is None else summed + product
        out_ref[g] = (summed / total).astype(out_ref.dtype)
        lse = top + jnp.log(total)
        wide = jnp.broadcast_to(lse, (lse.shape[0], 128))
        lse_ref[g] = jnp.transpose(wide)[:STAT_ROWS]


def attend_partial(flags, query_block, key_blocks, value_blocks, out_dtype):
    nsrc = len(key_blocks)
    rows, width = query_block.shape
    block_rows = key_blocks[0].shape[0]
    nheads = width // HEAD_DIM
    group = max(g for g in range(1, 6) if nheads % g == 0)
    row_tile = rows // ROW_SPLIT
    span = group * HEAD_DIM
    q_spec = pl.BlockSpec((row_tile, span), lambda h, r, f: (r, h))
    kv_spec = pl.BlockSpec((block_rows, span), lambda h, r, f: (0, h))
    out_spec = pl.BlockSpec((group, row_tile, HEAD_DIM), lambda h, r, f: (h, r, 0))
    lse_spec = pl.BlockSpec((group, STAT_ROWS, row_tile), lambda h, r, f: (h, 0, r))
    grid_spec = pltpu.PrefetchScalarGridSpec(
        num_scalar_prefetch=1,
        grid=(nheads // group, ROW_SPLIT),
        in_specs=[q_spec] + [kv_spec] * (2 * nsrc),
        out_specs=[out_spec, lse_spec],
        scratch_shapes=[pltpu.VMEM((nsrc, row_tile, block_rows), jnp.float32)],
    )
    return pl.pallas_call(
        lambda *a: partial_kernel(nsrc, group, *a),
        grid_spec=grid_spec,
        out_shape=[
            jax.ShapeDtypeStruct((nheads, rows, HEAD_DIM), out_dtype),
            jax.ShapeDtypeStruct((nheads, STAT_ROWS, rows), jnp.float32),
        ],
        compiler_params=pltpu.CompilerParams(dimension_semantics=("parallel", "arbitrary")),
    )(flags, query_block, *key_blocks, *value_blocks)


def membership(listed, block_ids, valid):
    hit = jnp.any(listed[None, :] == jnp.stack(block_ids)[:, None], axis=1)
    return (hit & jnp.stack(valid)).astype(jnp.int32)


def local(queries, new_keys, new_values, cache_keys, cache_values, sources):
    head_width = new_keys.shape[1]
    nheads = head_width // HEAD_DIM
    sp_count = lax.axis_size("sp")
    sp_place = lax.axis_index("sp")
    seq_count = lax.axis_size("seq")
    s = lax.axis_index("seq")
    chips = seq_count // 2
    chip = s // 2
    other = s ^ 1
    listed = sources[0]

    query_parts = [lax.dynamic_slice_in_dim(queries, sp_place * head_width, head_width, 1)]
    for d in range(1, sp_count):
        columns = ((sp_place + d) % sp_count) * head_width
        piece = lax.dynamic_slice_in_dim(queries, columns, head_width, 1)
        query_parts.append(
            lax.ppermute(piece, "sp", [(i, (i + d) % sp_count) for i in range(sp_count)])
        )
    query_block = jnp.concatenate(query_parts, axis=0)

    back = [(i, (i - 2) % seq_count) for i in range(seq_count)]
    forth = [(i, (i + 2) % seq_count) for i in range(seq_count)]
    t = (s - 2) % seq_count
    t_chip = t // 2
    remote_ids = [seq_count + t, seq_count + (t ^ 1), t, t ^ 1]
    remote_valid = [
        s >= 2,
        s >= 2,
        (t_chip == 0) | (t_chip == chips - 1),
        (t_chip == 0) | (t_chip == chips - 1),
    ]
    if chips > 2:
        remote_ids += [t % 2, 1 - t % 2]
        remote_valid += [(t_chip >= 1) & (t_chip <= chips - 2)] * 2
    remote_flags = membership(listed, remote_ids, remote_valid)
    half = query_block.shape[0] // 2
    got_flags = lax.ppermute(remote_flags, "seq", back)
    got_halves = [
        lax.ppermute(query_block[:half], "seq", back),
        lax.ppermute(query_block[half:], "seq", back),
    ]

    swap = [(i, i ^ 1) for i in range(seq_count)]
    partner_k, partner_v, partner_ck, partner_cv = lax.ppermute(
        (new_keys, new_values, cache_keys, cache_values), "seq", swap
    )
    keys = [new_keys, partner_k, cache_keys, partner_ck]
    values = [new_values, partner_v, cache_values, partner_cv]

    if chips > 2:
        first = (cache_keys, cache_values)
        span = 1
        while span < chips - 1:
            pairs = [
                (2 * c + k, 2 * (c + span) + k)
                for c in range(span)
                if c + span < chips - 1
                for k in range(2)
            ]
            got = lax.ppermute(first, "seq", pairs)
            taking = (chip >= span) & (chip < 2 * span)
            first = tuple(jnp.where(taking, b, a) for a, b in zip(first, got))
            span *= 2
        first_other = lax.ppermute(first, "seq", swap)
        remote_keys = keys + [first[0], first_other[0]]
        remote_values = values + [first[1], first_other[1]]
    else:
        remote_keys, remote_values = keys, values

    local_flags = membership(
        listed,
        [seq_count + s, seq_count + other, s, other],
        [s >= 0, s >= 0, chip == 0, chip == 0],
    )
    local_out, local_lse = attend_partial(local_flags, query_block, keys, values, jnp.float32)

    mixed_halves = []
    for k, got_query in enumerate(got_halves):
        far_out, far_lse = attend_partial(
            got_flags, got_query, remote_keys, remote_values, jnp.bfloat16
        )
        far_out, far_lse = lax.ppermute((far_out, far_lse), "seq", forth)
        near = slice(k * half, (k + 1) * half)
        lse_a = local_lse[:, 0, near][:, :, None]
        lse_b = far_lse[:, 0, :][:, :, None]
        top = jnp.maximum(lse_a, lse_b)
        weight_a = jnp.exp(lse_a - top)
        weight_b = jnp.exp(lse_b - top)
        mixed = (
            local_out[:, near] * weight_a + far_out.astype(jnp.float32) * weight_b
        ) / (weight_a + weight_b)
        mixed_halves.append(mixed.astype(jnp.bfloat16))
    rows_all = query_block.shape[0]
    heads_out = jnp.transpose(jnp.concatenate(mixed_halves, axis=1), (1, 0, 2)).reshape(
        rows_all, head_width
    )

    rows = queries.shape[0]
    result = jnp.zeros((rows, queries.shape[1]), jnp.bfloat16)
    for d in range(sp_count):
        piece = heads_out[d * rows : (d + 1) * rows]
        if d:
            piece = lax.ppermute(piece, "sp", [(i, (i - d) % sp_count) for i in range(sp_count)])
        columns = ((sp_place + d) % sp_count) * head_width
        result = lax.dynamic_update_slice_in_dim(result, piece, columns, 1)
    return result


def solution(mesh):
    return jax.shard_map(
        local,
        mesh=mesh,
        in_specs=(
            P(("groups", "seq", "sp"), None),
            P(("groups", "seq"), "sp"),
            P(("groups", "seq"), "sp"),
            P(("groups", "seq"), "sp"),
            P(("groups", "seq"), "sp"),
            P(("groups", "seq"), None),
        ),
        out_specs=P(("groups", "seq", "sp"), None),
        check_vma=False,
    )
```

```python
import math

import jax
import jax.numpy as jnp
from jax import lax
from jax.experimental import pallas as pl
from jax.experimental.pallas import tpu as pltpu
from jax.sharding import PartitionSpec as P

HEAD_DIM = 128
ROW_SPLIT = 2
STAT_ROWS = 8


def partial_kernel(nsrc, group, flags_ref, q_ref, *refs):
    key_refs = refs[:nsrc]
    value_refs = refs[nsrc : 2 * nsrc]
    out_ref, lse_ref = refs[2 * nsrc : 2 * nsrc + 2]
    score_ref = refs[2 * nsrc + 2]
    score_scale = 1.0 / math.sqrt(HEAD_DIM)
    for g in range(group):
        cols = slice(g * HEAD_DIM, (g + 1) * HEAD_DIM)
        query = q_ref[:, cols]
        top = None
        for j in range(nsrc):
            scores = lax.dot_general(
                query,
                key_refs[j][:, cols],
                (((1,), (1,)), ((), ())),
                preferred_element_type=jnp.float32,
            ) * score_scale
            scores = jnp.where(flags_ref[j] > 0, scores, -1e30)
            score_ref[j] = scores
            block_top = jnp.max(scores, axis=1, keepdims=True)
            top = block_top if top is None else jnp.maximum(top, block_top)
        total = None
        summed = None
        for j in range(nsrc):
            weights = jnp.exp(score_ref[j] - top)
            part_total = jnp.sum(weights, axis=1, keepdims=True)
            product = jnp.dot(
                weights.astype(jnp.bfloat16), value_refs[j][:, cols], preferred_element_type=jnp.float32
            )
            total = part_total if total is None else total + part_total
            summed = product if summed is None else summed + product
        out_ref[g] = (summed / total).astype(out_ref.dtype)
        lse = top + jnp.log(total)
        wide = jnp.broadcast_to(lse, (lse.shape[0], 128))
        lse_ref[g] = jnp.transpose(wide)[:STAT_ROWS]


def attend_partial(flags, query_block, key_blocks, value_blocks, out_dtype, parts=1, part=0):
    nsrc = len(key_blocks)
    rows, width = query_block.shape
    rows = rows // parts
    block_rows = key_blocks[0].shape[0]
    nheads = width // HEAD_DIM
    group = max(g for g in range(1, 6) if nheads % g == 0)
    row_tile = rows // ROW_SPLIT
    span = group * HEAD_DIM
    q_spec = pl.BlockSpec((row_tile, span), lambda h, r, f: (r + part * ROW_SPLIT, h))
    kv_spec = pl.BlockSpec((block_rows, span), lambda h, r, f: (0, h))
    out_spec = pl.BlockSpec((group, row_tile, HEAD_DIM), lambda h, r, f: (h, r, 0))
    lse_spec = pl.BlockSpec((group, STAT_ROWS, row_tile), lambda h, r, f: (h, 0, r))
    grid_spec = pltpu.PrefetchScalarGridSpec(
        num_scalar_prefetch=1,
        grid=(nheads // group, ROW_SPLIT),
        in_specs=[q_spec] + [kv_spec] * (2 * nsrc),
        out_specs=[out_spec, lse_spec],
        scratch_shapes=[pltpu.VMEM((nsrc, row_tile, block_rows), jnp.float32)],
    )
    return pl.pallas_call(
        lambda *a: partial_kernel(nsrc, group, *a),
        grid_spec=grid_spec,
        out_shape=[
            jax.ShapeDtypeStruct((nheads, rows, HEAD_DIM), out_dtype),
            jax.ShapeDtypeStruct((nheads, STAT_ROWS, rows), jnp.float32),
        ],
        compiler_params=pltpu.CompilerParams(dimension_semantics=("parallel", "arbitrary")),
    )(flags, query_block, *key_blocks, *value_blocks)


def membership(listed, block_ids, valid):
    hit = jnp.any(listed[None, :] == jnp.stack(block_ids)[:, None], axis=1)
    return (hit & jnp.stack(valid)).astype(jnp.int32)


def local(queries, new_keys, new_values, cache_keys, cache_values, sources):
    head_width = new_keys.shape[1]
    nheads = head_width // HEAD_DIM
    sp_count = lax.axis_size("sp")
    sp_place = lax.axis_index("sp")
    seq_count = lax.axis_size("seq")
    s = lax.axis_index("seq")
    chips = seq_count // 2
    chip = s // 2
    other = s ^ 1
    listed = sources[0]

    query_parts = [lax.dynamic_slice_in_dim(queries, sp_place * head_width, head_width, 1)]
    for d in range(1, sp_count):
        columns = ((sp_place + d) % sp_count) * head_width
        piece = lax.dynamic_slice_in_dim(queries, columns, head_width, 1)
        query_parts.append(
            lax.ppermute(piece, "sp", [(i, (i + d) % sp_count) for i in range(sp_count)])
        )
    query_block = jnp.concatenate(query_parts, axis=0)

    back = [(i, (i - 2) % seq_count) for i in range(seq_count)]
    forth = [(i, (i + 2) % seq_count) for i in range(seq_count)]
    t = (s - 2) % seq_count
    t_chip = t // 2
    remote_ids = [seq_count + t, seq_count + (t ^ 1), t, t ^ 1]
    remote_valid = [
        s >= 2,
        s >= 2,
        (t_chip == 0) | (t_chip == chips - 1),
        (t_chip == 0) | (t_chip == chips - 1),
    ]
    if chips > 2:
        remote_ids += [t % 2, 1 - t % 2]
        remote_valid += [(t_chip >= 1) & (t_chip <= chips - 2)] * 2
    remote_flags = membership(listed, remote_ids, remote_valid)
    half = query_block.shape[0] // 2
    got_flags = lax.ppermute(remote_flags, "seq", back)
    got_halves = [
        lax.ppermute(query_block[:half], "seq", back),
        lax.ppermute(query_block[half:], "seq", back),
    ]

    swap = [(i, i ^ 1) for i in range(seq_count)]
    partner_k, partner_v, partner_ck, partner_cv = lax.ppermute(
        (new_keys, new_values, cache_keys, cache_values), "seq", swap
    )
    keys = [new_keys, partner_k, cache_keys, partner_ck]
    values = [new_values, partner_v, cache_values, partner_cv]

    if chips > 2:
        first = (cache_keys, cache_values)
        span = 1
        while span < chips - 1:
            pairs = [
                (2 * c + k, 2 * (c + span) + k)
                for c in range(span)
                if c + span < chips - 1
                for k in range(2)
            ]
            got = lax.ppermute(first, "seq", pairs)
            taking = (chip >= span) & (chip < 2 * span)
            first = tuple(jnp.where(taking, b, a) for a, b in zip(first, got))
            span *= 2
        first_other = lax.ppermute(first, "seq", swap)
        remote_keys = keys + [first[0], first_other[0]]
        remote_values = values + [first[1], first_other[1]]
    else:
        remote_keys, remote_values = keys, values

    local_flags = membership(
        listed,
        [seq_count + s, seq_count + other, s, other],
        [s >= 0, s >= 0, chip == 0, chip == 0],
    )
    local_parts = [
        attend_partial(local_flags, query_block, keys, values, jnp.float32, 2, k) for k in range(2)
    ]
    got_first, first_out, first_lse = lax.optimization_barrier(
        (got_halves[0], local_parts[0][0], local_parts[0][1])
    )
    got_halves = [got_first, got_halves[1]]
    local_parts = [(first_out, first_lse), local_parts[1]]

    mixed_halves = []
    for k, got_query in enumerate(got_halves):
        far_out, far_lse = attend_partial(
            got_flags, got_query, remote_keys, remote_values, jnp.bfloat16
        )
        far_out, far_lse = lax.ppermute((far_out, far_lse), "seq", forth)
        local_out, local_lse = local_parts[k]
        lse_a = local_lse[:, 0, :][:, :, None]
        lse_b = far_lse[:, 0, :][:, :, None]
        top = jnp.maximum(lse_a, lse_b)
        weight_a = jnp.exp(lse_a - top)
        weight_b = jnp.exp(lse_b - top)
        mixed = (
            local_out * weight_a + far_out.astype(jnp.float32) * weight_b
        ) / (weight_a + weight_b)
        mixed_halves.append(
            jnp.transpose(mixed.astype(jnp.bfloat16), (1, 0, 2)).reshape(half, head_width)
        )

    rows = queries.shape[0]
    result = jnp.zeros((rows, queries.shape[1]), jnp.bfloat16)
    for d in range(sp_count):
        start = d * rows
        piece = mixed_halves[start // half][start % half : start % half + rows]
        if d:
            piece = lax.ppermute(piece, "sp", [(i, (i - d) % sp_count) for i in range(sp_count)])
        columns = ((sp_place + d) % sp_count) * head_width
        result = lax.dynamic_update_slice_in_dim(result, piece, columns, 1)
    return result


def solution(mesh):
    return jax.shard_map(
        local,
        mesh=mesh,
        in_specs=(
            P(("groups", "seq", "sp"), None),
            P(("groups", "seq"), "sp"),
            P(("groups", "seq"), "sp"),
            P(("groups", "seq"), "sp"),
            P(("groups", "seq"), "sp"),
            P(("groups", "seq"), None),
        ),
        out_specs=P(("groups", "seq", "sp"), None),
        check_vma=False,
    )
```

```python
import math

import jax
import jax.numpy as jnp
from jax import lax
from jax.experimental import pallas as pl
from jax.experimental.pallas import tpu as pltpu
from jax.sharding import PartitionSpec as P

HEAD_DIM = 128
ROW_SPLIT = 2
STAT_ROWS = 8


def partial_kernel(nsrc, group, flags_ref, q_ref, *refs):
    key_refs = refs[:nsrc]
    value_refs = refs[nsrc : 2 * nsrc]
    out_ref, lse_ref = refs[2 * nsrc : 2 * nsrc + 2]
    score_ref = refs[2 * nsrc + 2]
    score_scale = 1.0 / math.sqrt(HEAD_DIM)
    for g in range(group):
        cols = slice(g * HEAD_DIM, (g + 1) * HEAD_DIM)
        query = q_ref[:, cols]
        top = None
        for j in range(nsrc):
            scores = lax.dot_general(
                query,
                key_refs[j][:, cols],
                (((1,), (1,)), ((), ())),
                preferred_element_type=jnp.float32,
            ) * score_scale
            scores = jnp.where(flags_ref[j] > 0, scores, -1e30)
            score_ref[j] = scores
            block_top = jnp.max(scores, axis=1, keepdims=True)
            top = block_top if top is None else jnp.maximum(top, block_top)
        total = None
        summed = None
        for j in range(nsrc):
            weights = jnp.exp(score_ref[j] - top)
            part_total = jnp.sum(weights, axis=1, keepdims=True)
            product = jnp.dot(
                weights.astype(jnp.bfloat16), value_refs[j][:, cols], preferred_element_type=jnp.float32
            )
            total = part_total if total is None else total + part_total
            summed = product if summed is None else summed + product
        out_ref[g] = (summed / total).astype(out_ref.dtype)
        lse = top + jnp.log(total)
        wide = jnp.broadcast_to(lse, (lse.shape[0], 128))
        lse_ref[g] = jnp.transpose(wide)[:STAT_ROWS]


def attend_partial(flags, query_block, key_blocks, value_blocks, out_dtype):
    nsrc = len(key_blocks)
    rows, width = query_block.shape
    block_rows = key_blocks[0].shape[0]
    nheads = width // HEAD_DIM
    group = max(g for g in range(1, 6) if nheads % g == 0)
    split = ROW_SPLIT if (rows // ROW_SPLIT) % 128 == 0 else 1
    row_tile = rows // split
    span = group * HEAD_DIM
    q_spec = pl.BlockSpec((row_tile, span), lambda h, r, f: (r, h))
    kv_spec = pl.BlockSpec((block_rows, span), lambda h, r, f: (0, h))
    out_spec = pl.BlockSpec((group, row_tile, HEAD_DIM), lambda h, r, f: (h, r, 0))
    lse_spec = pl.BlockSpec((group, STAT_ROWS, row_tile), lambda h, r, f: (h, 0, r))
    grid_spec = pltpu.PrefetchScalarGridSpec(
        num_scalar_prefetch=1,
        grid=(nheads // group, split),
        in_specs=[q_spec] + [kv_spec] * (2 * nsrc),
        out_specs=[out_spec, lse_spec],
        scratch_shapes=[pltpu.VMEM((nsrc, row_tile, block_rows), jnp.float32)],
    )
    return pl.pallas_call(
        lambda *a: partial_kernel(nsrc, group, *a),
        grid_spec=grid_spec,
        out_shape=[
            jax.ShapeDtypeStruct((nheads, rows, HEAD_DIM), out_dtype),
            jax.ShapeDtypeStruct((nheads, STAT_ROWS, rows), jnp.float32),
        ],
        compiler_params=pltpu.CompilerParams(dimension_semantics=("parallel", "arbitrary")),
    )(flags, query_block, *key_blocks, *value_blocks)


def membership(listed, block_ids, valid):
    hit = jnp.any(listed[None, :] == jnp.stack(block_ids)[:, None], axis=1)
    return (hit & jnp.stack(valid)).astype(jnp.int32)


def local(queries, new_keys, new_values, cache_keys, cache_values, sources):
    head_width = new_keys.shape[1]
    nheads = head_width // HEAD_DIM
    sp_count = lax.axis_size("sp")
    sp_place = lax.axis_index("sp")
    seq_count = lax.axis_size("seq")
    s = lax.axis_index("seq")
    chips = seq_count // 2
    chip = s // 2
    other = s ^ 1
    listed = sources[0]

    query_parts = [lax.dynamic_slice_in_dim(queries, sp_place * head_width, head_width, 1)]
    for d in range(1, sp_count):
        columns = ((sp_place + d) % sp_count) * head_width
        piece = lax.dynamic_slice_in_dim(queries, columns, head_width, 1)
        query_parts.append(
            lax.ppermute(piece, "sp", [(i, (i + d) % sp_count) for i in range(sp_count)])
        )
    query_block = jnp.concatenate(query_parts, axis=0)

    back = [(i, (i - 2) % seq_count) for i in range(seq_count)]
    forth = [(i, (i + 2) % seq_count) for i in range(seq_count)]
    t = (s - 2) % seq_count
    t_chip = t // 2
    remote_ids = [seq_count + t, seq_count + (t ^ 1), t, t ^ 1]
    remote_valid = [
        s >= 2,
        s >= 2,
        (t_chip == 0) | (t_chip == chips - 1),
        (t_chip == 0) | (t_chip == chips - 1),
    ]
    if chips > 2:
        remote_ids += [t % 2, 1 - t % 2]
        remote_valid += [(t_chip >= 1) & (t_chip <= chips - 2)] * 2
    remote_flags = membership(listed, remote_ids, remote_valid)
    rows = queries.shape[0]
    got_flags = lax.ppermute(remote_flags, "seq", back)
    got_halves = [
        lax.ppermute(query_parts[0], "seq", back),
        lax.ppermute(jnp.concatenate(query_parts[1:], axis=0), "seq", back),
    ]
    bounds = [(0, rows), (rows, query_parts[0].shape[0] * sp_count)]

    swap = [(i, i ^ 1) for i in range(seq_count)]
    partner_k, partner_v, partner_ck, partner_cv = lax.ppermute(
        (new_keys, new_values, cache_keys, cache_values), "seq", swap
    )
    keys = [new_keys, partner_k, cache_keys, partner_ck]
    values = [new_values, partner_v, cache_values, partner_cv]

    if chips > 2:
        first = (cache_keys, cache_values)
        span = 1
        while span < chips - 1:
            pairs = [
                (2 * c + k, 2 * (c + span) + k)
                for c in range(span)
                if c + span < chips - 1
                for k in range(2)
            ]
            got = lax.ppermute(first, "seq", pairs)
            taking = (chip >= span) & (chip < 2 * span)
            first = tuple(jnp.where(taking, b, a) for a, b in zip(first, got))
            span *= 2
        first_other = lax.ppermute(first, "seq", swap)
        remote_keys = keys + [first[0], first_other[0]]
        remote_values = values + [first[1], first_other[1]]
    else:
        remote_keys, remote_values = keys, values

    local_flags = membership(
        listed,
        [seq_count + s, seq_count + other, s, other],
        [s >= 0, s >= 0, chip == 0, chip == 0],
    )
    local_out, local_lse = attend_partial(local_flags, query_block, keys, values, jnp.float32)

    mixed_halves = []
    for k, got_query in enumerate(got_halves):
        far_out, far_lse = attend_partial(
            got_flags, got_query, remote_keys, remote_values, jnp.bfloat16
        )
        far_out, far_lse = lax.ppermute((far_out, far_lse), "seq", forth)
        near = slice(*bounds[k])
        lse_a = local_lse[:, 0, near][:, :, None]
        lse_b = far_lse[:, 0, :][:, :, None]
        top = jnp.maximum(lse_a, lse_b)
        weight_a = jnp.exp(lse_a - top)
        weight_b = jnp.exp(lse_b - top)
        mixed = (
            local_out[:, near] * weight_a + far_out.astype(jnp.float32) * weight_b
        ) / (weight_a + weight_b)
        mixed_halves.append(
            jnp.transpose(mixed.astype(jnp.bfloat16), (1, 0, 2)).reshape(-1, head_width)
        )

    result = jnp.zeros((rows, queries.shape[1]), jnp.bfloat16)
    for d in range(sp_count):
        if d:
            piece = mixed_halves[1][(d - 1) * rows : d * rows]
        else:
            piece = mixed_halves[0]
        if d:
            piece = lax.ppermute(piece, "sp", [(i, (i - d) % sp_count) for i in range(sp_count)])
        columns = ((sp_place + d) % sp_count) * head_width
        result = lax.dynamic_update_slice_in_dim(result, piece, columns, 1)
    return result


def solution(mesh):
    return jax.shard_map(
        local,
        mesh=mesh,
        in_specs=(
            P(("groups", "seq", "sp"), None),
            P(("groups", "seq"), "sp"),
            P(("groups", "seq"), "sp"),
            P(("groups", "seq"), "sp"),
            P(("groups", "seq"), "sp"),
            P(("groups", "seq"), None),
        ),
        out_specs=P(("groups", "seq", "sp"), None),
        check_vma=False,
    )
```

```python
import math

import jax
import jax.numpy as jnp
from jax import lax
from jax.experimental import pallas as pl
from jax.experimental.pallas import tpu as pltpu
from jax.sharding import PartitionSpec as P

HEAD_DIM = 128
ROW_SPLIT = 2
STAT_ROWS = 8


def partial_kernel(nsrc, group, flags_ref, q_ref, *refs):
    key_refs = refs[:nsrc]
    value_refs = refs[nsrc : 2 * nsrc]
    out_ref, lse_ref = refs[2 * nsrc : 2 * nsrc + 2]
    score_ref = refs[2 * nsrc + 2]
    score_scale = 1.0 / math.sqrt(HEAD_DIM)
    for g in range(group):
        cols = slice(g * HEAD_DIM, (g + 1) * HEAD_DIM)
        query = q_ref[:, cols]
        top = None
        for j in range(nsrc):
            scores = lax.dot_general(
                query,
                key_refs[j][:, cols],
                (((1,), (1,)), ((), ())),
                preferred_element_type=jnp.float32,
            ) * score_scale
            scores = jnp.where(flags_ref[j] > 0, scores, -1e30)
            score_ref[j] = scores
            block_top = jnp.max(scores, axis=1, keepdims=True)
            top = block_top if top is None else jnp.maximum(top, block_top)
        total = None
        summed = None
        for j in range(nsrc):
            weights = jnp.exp(score_ref[j] - top)
            part_total = jnp.sum(weights, axis=1, keepdims=True)
            product = jnp.dot(
                weights.astype(jnp.bfloat16), value_refs[j][:, cols], preferred_element_type=jnp.float32
            )
            total = part_total if total is None else total + part_total
            summed = product if summed is None else summed + product
        out_ref[g] = (summed / total).astype(out_ref.dtype)
        lse = top + jnp.log(total)
        wide = jnp.broadcast_to(lse, (lse.shape[0], 128))
        lse_ref[g] = jnp.transpose(wide)[:STAT_ROWS]


def attend_partial(flags, query_block, key_blocks, value_blocks, out_dtype):
    nsrc = len(key_blocks)
    rows, width = query_block.shape
    block_rows = key_blocks[0].shape[0]
    nheads = width // HEAD_DIM
    group = max(g for g in range(1, 6) if nheads % g == 0)
    split = ROW_SPLIT if (rows // ROW_SPLIT) % 128 == 0 else 1
    row_tile = rows // split
    span = group * HEAD_DIM
    q_spec = pl.BlockSpec((row_tile, span), lambda h, r, f: (r, h))
    kv_spec = pl.BlockSpec((block_rows, span), lambda h, r, f: (0, h))
    out_spec = pl.BlockSpec((group, row_tile, HEAD_DIM), lambda h, r, f: (h, r, 0))
    lse_spec = pl.BlockSpec((group, STAT_ROWS, row_tile), lambda h, r, f: (h, 0, r))
    grid_spec = pltpu.PrefetchScalarGridSpec(
        num_scalar_prefetch=1,
        grid=(nheads // group, split),
        in_specs=[q_spec] + [kv_spec] * (2 * nsrc),
        out_specs=[out_spec, lse_spec],
        scratch_shapes=[pltpu.VMEM((nsrc, row_tile, block_rows), jnp.float32)],
    )
    return pl.pallas_call(
        lambda *a: partial_kernel(nsrc, group, *a),
        grid_spec=grid_spec,
        out_shape=[
            jax.ShapeDtypeStruct((nheads, rows, HEAD_DIM), out_dtype),
            jax.ShapeDtypeStruct((nheads, STAT_ROWS, rows), jnp.float32),
        ],
        compiler_params=pltpu.CompilerParams(dimension_semantics=("parallel", "arbitrary")),
    )(flags, query_block, *key_blocks, *value_blocks)


def membership(listed, block_ids, valid):
    hit = jnp.any(listed[None, :] == jnp.stack(block_ids)[:, None], axis=1)
    return (hit & jnp.stack(valid)).astype(jnp.int32)


def local(queries, new_keys, new_values, cache_keys, cache_values, sources):
    head_width = new_keys.shape[1]
    nheads = head_width // HEAD_DIM
    sp_count = lax.axis_size("sp")
    sp_place = lax.axis_index("sp")
    seq_count = lax.axis_size("seq")
    s = lax.axis_index("seq")
    chips = seq_count // 2
    chip = s // 2
    other = s ^ 1
    listed = sources[0]

    query_parts = [lax.dynamic_slice_in_dim(queries, sp_place * head_width, head_width, 1)]
    for d in range(1, sp_count):
        columns = ((sp_place + d) % sp_count) * head_width
        piece = lax.dynamic_slice_in_dim(queries, columns, head_width, 1)
        query_parts.append(
            lax.ppermute(piece, "sp", [(i, (i + d) % sp_count) for i in range(sp_count)])
        )
    query_block = jnp.concatenate(query_parts, axis=0)

    back = [(i, (i - 2) % seq_count) for i in range(seq_count)]
    forth = [(i, (i + 2) % seq_count) for i in range(seq_count)]
    t = (s - 2) % seq_count
    t_chip = t // 2
    remote_ids = [seq_count + t, seq_count + (t ^ 1), t, t ^ 1]
    remote_valid = [
        s >= 2,
        s >= 2,
        (t_chip == 0) | (t_chip == chips - 1),
        (t_chip == 0) | (t_chip == chips - 1),
    ]
    if chips > 2:
        remote_ids += [t % 2, 1 - t % 2]
        remote_valid += [(t_chip >= 1) & (t_chip <= chips - 2)] * 2
    remote_flags = membership(listed, remote_ids, remote_valid)
    rows = queries.shape[0]
    got_flags = lax.ppermute(remote_flags, "seq", back)
    got_first = lax.ppermute(query_parts[0], "seq", back)
    got_first, rest = lax.optimization_barrier(
        (got_first, jnp.concatenate(query_parts[1:], axis=0))
    )
    got_halves = [got_first, lax.ppermute(rest, "seq", back)]
    bounds = [(0, rows), (rows, query_parts[0].shape[0] * sp_count)]

    swap = [(i, i ^ 1) for i in range(seq_count)]
    partner_k, partner_v, partner_ck, partner_cv = lax.ppermute(
        (new_keys, new_values, cache_keys, cache_values), "seq", swap
    )
    keys = [new_keys, partner_k, cache_keys, partner_ck]
    values = [new_values, partner_v, cache_values, partner_cv]

    if chips > 2:
        first = (cache_keys, cache_values)
        span = 1
        while span < chips - 1:
            pairs = [
                (2 * c + k, 2 * (c + span) + k)
                for c in range(span)
                if c + span < chips - 1
                for k in range(2)
            ]
            got = lax.ppermute(first, "seq", pairs)
            taking = (chip >= span) & (chip < 2 * span)
            first = tuple(jnp.where(taking, b, a) for a, b in zip(first, got))
            span *= 2
        first_other = lax.ppermute(first, "seq", swap)
        remote_keys = keys + [first[0], first_other[0]]
        remote_values = values + [first[1], first_other[1]]
    else:
        remote_keys, remote_values = keys, values

    local_flags = membership(
        listed,
        [seq_count + s, seq_count + other, s, other],
        [s >= 0, s >= 0, chip == 0, chip == 0],
    )
    local_out, local_lse = attend_partial(local_flags, query_block, keys, values, jnp.float32)

    mixed_halves = []
    for k, got_query in enumerate(got_halves):
        far_out, far_lse = attend_partial(
            got_flags, got_query, remote_keys, remote_values, jnp.bfloat16
        )
        far_out, far_lse = lax.ppermute((far_out, far_lse), "seq", forth)
        near = slice(*bounds[k])
        lse_a = local_lse[:, 0, near][:, :, None]
        lse_b = far_lse[:, 0, :][:, :, None]
        top = jnp.maximum(lse_a, lse_b)
        weight_a = jnp.exp(lse_a - top)
        weight_b = jnp.exp(lse_b - top)
        mixed = (
            local_out[:, near] * weight_a + far_out.astype(jnp.float32) * weight_b
        ) / (weight_a + weight_b)
        mixed_halves.append(
            jnp.transpose(mixed.astype(jnp.bfloat16), (1, 0, 2)).reshape(-1, head_width)
        )

    result = jnp.zeros((rows, queries.shape[1]), jnp.bfloat16)
    for d in range(sp_count):
        if d:
            piece = mixed_halves[1][(d - 1) * rows : d * rows]
        else:
            piece = mixed_halves[0]
        if d:
            piece = lax.ppermute(piece, "sp", [(i, (i - d) % sp_count) for i in range(sp_count)])
        columns = ((sp_place + d) % sp_count) * head_width
        result = lax.dynamic_update_slice_in_dim(result, piece, columns, 1)
    return result


def solution(mesh):
    return jax.shard_map(
        local,
        mesh=mesh,
        in_specs=(
            P(("groups", "seq", "sp"), None),
            P(("groups", "seq"), "sp"),
            P(("groups", "seq"), "sp"),
            P(("groups", "seq"), "sp"),
            P(("groups", "seq"), "sp"),
            P(("groups", "seq"), None),
        ),
        out_specs=P(("groups", "seq", "sp"), None),
        check_vma=False,
    )
```

```python
import math

import jax
import jax.numpy as jnp
from jax import lax
from jax.experimental import pallas as pl
from jax.experimental.pallas import tpu as pltpu
from jax.sharding import PartitionSpec as P

HEAD_DIM = 128
ROW_SPLIT = 2
STAT_ROWS = 8


def partial_kernel(nsrc, group, flags_ref, q_ref, *refs):
    key_refs = refs[:nsrc]
    value_refs = refs[nsrc : 2 * nsrc]
    out_ref, lse_ref = refs[2 * nsrc : 2 * nsrc + 2]
    score_ref = refs[2 * nsrc + 2]
    score_scale = 1.0 / math.sqrt(HEAD_DIM)
    for g in range(group):
        cols = slice(g * HEAD_DIM, (g + 1) * HEAD_DIM)
        query = q_ref[:, cols]
        top = None
        for j in range(nsrc):
            scores = lax.dot_general(
                query,
                key_refs[j][:, cols],
                (((1,), (1,)), ((), ())),
                preferred_element_type=jnp.float32,
            ) * score_scale
            scores = jnp.where(flags_ref[j] > 0, scores, -1e30)
            score_ref[j] = scores
            block_top = jnp.max(scores, axis=1, keepdims=True)
            top = block_top if top is None else jnp.maximum(top, block_top)
        total = None
        summed = None
        for j in range(nsrc):
            weights = jnp.exp(score_ref[j] - top)
            part_total = jnp.sum(weights, axis=1, keepdims=True)
            product = jnp.dot(
                weights.astype(jnp.bfloat16), value_refs[j][:, cols], preferred_element_type=jnp.float32
            )
            total = part_total if total is None else total + part_total
            summed = product if summed is None else summed + product
        out_ref[g] = (summed / total).astype(out_ref.dtype)
        lse = top + jnp.log(total)
        wide = jnp.broadcast_to(lse, (lse.shape[0], 128))
        lse_ref[g] = jnp.transpose(wide)[:STAT_ROWS]


def attend_partial(flags, query_block, key_blocks, value_blocks, out_dtype):
    nsrc = len(key_blocks)
    rows, width = query_block.shape
    block_rows = key_blocks[0].shape[0]
    nheads = width // HEAD_DIM
    group = max(g for g in range(1, 6) if nheads % g == 0)
    row_tile = rows // ROW_SPLIT
    span = group * HEAD_DIM
    q_spec = pl.BlockSpec((row_tile, span), lambda h, r, f: (r, h))
    kv_spec = pl.BlockSpec((block_rows, span), lambda h, r, f: (0, h))
    out_spec = pl.BlockSpec((group, row_tile, HEAD_DIM), lambda h, r, f: (h, r, 0))
    lse_spec = pl.BlockSpec((group, STAT_ROWS, row_tile), lambda h, r, f: (h, 0, r))
    grid_spec = pltpu.PrefetchScalarGridSpec(
        num_scalar_prefetch=1,
        grid=(nheads // group, ROW_SPLIT),
        in_specs=[q_spec] + [kv_spec] * (2 * nsrc),
        out_specs=[out_spec, lse_spec],
        scratch_shapes=[pltpu.VMEM((nsrc, row_tile, block_rows), jnp.float32)],
    )
    return pl.pallas_call(
        lambda *a: partial_kernel(nsrc, group, *a),
        grid_spec=grid_spec,
        out_shape=[
            jax.ShapeDtypeStruct((nheads, rows, HEAD_DIM), out_dtype),
            jax.ShapeDtypeStruct((nheads, STAT_ROWS, rows), jnp.float32),
        ],
        compiler_params=pltpu.CompilerParams(dimension_semantics=("parallel", "arbitrary")),
    )(flags, query_block, *key_blocks, *value_blocks)


def membership(listed, block_ids, valid):
    hit = jnp.any(listed[None, :] == jnp.stack(block_ids)[:, None], axis=1)
    return (hit & jnp.stack(valid)).astype(jnp.int32)


def local(queries, new_keys, new_values, cache_keys, cache_values, sources):
    head_width = new_keys.shape[1]
    nheads = head_width // HEAD_DIM
    sp_count = lax.axis_size("sp")
    sp_place = lax.axis_index("sp")
    seq_count = lax.axis_size("seq")
    s = lax.axis_index("seq")
    chips = seq_count // 2
    chip = s // 2
    other = s ^ 1
    listed = sources[0]

    query_parts = [lax.dynamic_slice_in_dim(queries, sp_place * head_width, head_width, 1)]
    for d in range(1, sp_count):
        columns = ((sp_place + d) % sp_count) * head_width
        piece = lax.dynamic_slice_in_dim(queries, columns, head_width, 1)
        query_parts.append(
            lax.ppermute(piece, "sp", [(i, (i + d) % sp_count) for i in range(sp_count)])
        )
    query_block = jnp.concatenate(query_parts, axis=0)

    back = [(i, (i - 2) % seq_count) for i in range(seq_count)]
    forth = [(i, (i + 2) % seq_count) for i in range(seq_count)]
    t = (s - 2) % seq_count
    t_chip = t // 2
    remote_ids = [seq_count + t, seq_count + (t ^ 1), t, t ^ 1]
    remote_valid = [
        s >= 2,
        s >= 2,
        (t_chip == 0) | (t_chip == chips - 1),
        (t_chip == 0) | (t_chip == chips - 1),
    ]
    if chips > 2:
        remote_ids += [t % 2, 1 - t % 2]
        remote_valid += [(t_chip >= 1) & (t_chip <= chips - 2)] * 2
    remote_flags = membership(listed, remote_ids, remote_valid)
    half = query_block.shape[0] // 2
    got_first, got_flags = lax.ppermute((query_block[:half], remote_flags), "seq", back)
    got_halves = [got_first, lax.ppermute(query_block[half:], "seq", back)]

    swap = [(i, i ^ 1) for i in range(seq_count)]
    partner_k, partner_v, partner_ck, partner_cv = lax.ppermute(
        (new_keys, new_values, cache_keys, cache_values), "seq", swap
    )
    keys = [new_keys, partner_k, cache_keys, partner_ck]
    values = [new_values, partner_v, cache_values, partner_cv]

    if chips > 2:
        first = (cache_keys, cache_values)
        span = 1
        while span < chips - 1:
            pairs = [
                (2 * c + k, 2 * (c + span) + k)
                for c in range(span)
                if c + span < chips - 1
                for k in range(2)
            ]
            got = lax.ppermute(first, "seq", pairs)
            taking = (chip >= span) & (chip < 2 * span)
            first = tuple(jnp.where(taking, b, a) for a, b in zip(first, got))
            span *= 2
        first_other = lax.ppermute(first, "seq", swap)
        remote_keys = keys + [first[0], first_other[0]]
        remote_values = values + [first[1], first_other[1]]
    else:
        remote_keys, remote_values = keys, values

    local_flags = membership(
        listed,
        [seq_count + s, seq_count + other, s, other],
        [s >= 0, s >= 0, chip == 0, chip == 0],
    )
    local_out, local_lse = attend_partial(local_flags, query_block, keys, values, jnp.float32)
    got_first, local_out, local_lse = lax.optimization_barrier((got_halves[0], local_out, local_lse))
    got_halves = [got_first, got_halves[1]]

    mixed_halves = []
    for k, got_query in enumerate(got_halves):
        far_out, far_lse = attend_partial(
            got_flags, got_query, remote_keys, remote_values, jnp.bfloat16
        )
        far_out, far_lse = lax.ppermute((far_out, far_lse), "seq", forth)
        near = slice(k * half, (k + 1) * half)
        lse_a = local_lse[:, 0, near][:, :, None]
        lse_b = far_lse[:, 0, :][:, :, None]
        top = jnp.maximum(lse_a, lse_b)
        weight_a = jnp.exp(lse_a - top)
        weight_b = jnp.exp(lse_b - top)
        mixed = (
            local_out[:, near] * weight_a + far_out.astype(jnp.float32) * weight_b
        ) / (weight_a + weight_b)
        mixed_halves.append(mixed.astype(jnp.bfloat16))
    rows_all = query_block.shape[0]
    heads_out = jnp.transpose(jnp.concatenate(mixed_halves, axis=1), (1, 0, 2)).reshape(
        rows_all, head_width
    )

    rows = queries.shape[0]
    result = jnp.zeros((rows, queries.shape[1]), jnp.bfloat16)
    for d in range(sp_count):
        piece = heads_out[d * rows : (d + 1) * rows]
        if d:
            piece = lax.ppermute(piece, "sp", [(i, (i - d) % sp_count) for i in range(sp_count)])
        columns = ((sp_place + d) % sp_count) * head_width
        result = lax.dynamic_update_slice_in_dim(result, piece, columns, 1)
    return result


def solution(mesh):
    return jax.shard_map(
        local,
        mesh=mesh,
        in_specs=(
            P(("groups", "seq", "sp"), None),
            P(("groups", "seq"), "sp"),
            P(("groups", "seq"), "sp"),
            P(("groups", "seq"), "sp"),
            P(("groups", "seq"), "sp"),
            P(("groups", "seq"), None),
        ),
        out_specs=P(("groups", "seq", "sp"), None),
        check_vma=False,
    )
```

```python
import math

import jax
import jax.numpy as jnp
from jax import lax
from jax.experimental import pallas as pl
from jax.experimental.pallas import tpu as pltpu
from jax.sharding import PartitionSpec as P

HEAD_DIM = 128
ROW_SPLIT = 2
STAT_ROWS = 8


def partial_kernel(nsrc, group, flags_ref, q_ref, *refs):
    key_refs = refs[:nsrc]
    value_refs = refs[nsrc : 2 * nsrc]
    out_ref, lse_ref = refs[2 * nsrc : 2 * nsrc + 2]
    score_ref = refs[2 * nsrc + 2]
    score_scale = 1.0 / math.sqrt(HEAD_DIM)
    for g in range(group):
        cols = slice(g * HEAD_DIM, (g + 1) * HEAD_DIM)
        query = q_ref[:, cols]
        top = None
        for j in range(nsrc):
            scores = lax.dot_general(
                query,
                key_refs[j][:, cols],
                (((1,), (1,)), ((), ())),
                preferred_element_type=jnp.float32,
            ) * score_scale
            scores = jnp.where(flags_ref[j] > 0, scores, -1e30)
            score_ref[j] = scores
            block_top = jnp.max(scores, axis=1, keepdims=True)
            top = block_top if top is None else jnp.maximum(top, block_top)
        total = None
        summed = None
        for j in range(nsrc):
            weights = jnp.exp(score_ref[j] - top)
            part_total = jnp.sum(weights, axis=1, keepdims=True)
            product = jnp.dot(
                weights.astype(jnp.bfloat16), value_refs[j][:, cols], preferred_element_type=jnp.float32
            )
            total = part_total if total is None else total + part_total
            summed = product if summed is None else summed + product
        out_ref[g] = (summed / total).astype(out_ref.dtype)
        lse = top + jnp.log(total)
        wide = jnp.broadcast_to(lse, (lse.shape[0], 128))
        lse_ref[g] = jnp.transpose(wide)[:STAT_ROWS]


def attend_partial(flags, query_block, key_blocks, value_blocks, out_dtype):
    nsrc = len(key_blocks)
    rows, width = query_block.shape
    block_rows = key_blocks[0].shape[0]
    nheads = width // HEAD_DIM
    group = max(g for g in range(1, 6) if nheads % g == 0)
    row_tile = rows // ROW_SPLIT
    span = group * HEAD_DIM
    q_spec = pl.BlockSpec((row_tile, span), lambda h, r, f: (r, h))
    kv_spec = pl.BlockSpec((block_rows, span), lambda h, r, f: (0, h))
    out_spec = pl.BlockSpec((group, row_tile, HEAD_DIM), lambda h, r, f: (h, r, 0))
    lse_spec = pl.BlockSpec((group, STAT_ROWS, row_tile), lambda h, r, f: (h, 0, r))
    grid_spec = pltpu.PrefetchScalarGridSpec(
        num_scalar_prefetch=1,
        grid=(nheads // group, ROW_SPLIT),
        in_specs=[q_spec] + [kv_spec] * (2 * nsrc),
        out_specs=[out_spec, lse_spec],
        scratch_shapes=[pltpu.VMEM((nsrc, row_tile, block_rows), jnp.float32)],
    )
    return pl.pallas_call(
        lambda *a: partial_kernel(nsrc, group, *a),
        grid_spec=grid_spec,
        out_shape=[
            jax.ShapeDtypeStruct((nheads, rows, HEAD_DIM), out_dtype),
            jax.ShapeDtypeStruct((nheads, STAT_ROWS, rows), jnp.float32),
        ],
        compiler_params=pltpu.CompilerParams(dimension_semantics=("parallel", "arbitrary")),
    )(flags, query_block, *key_blocks, *value_blocks)


def membership(listed, block_ids, valid):
    hit = jnp.any(listed[None, :] == jnp.stack(block_ids)[:, None], axis=1)
    return (hit & jnp.stack(valid)).astype(jnp.int32)


def local(queries, new_keys, new_values, cache_keys, cache_values, sources):
    head_width = new_keys.shape[1]
    nheads = head_width // HEAD_DIM
    sp_count = lax.axis_size("sp")
    sp_place = lax.axis_index("sp")
    seq_count = lax.axis_size("seq")
    s = lax.axis_index("seq")
    chips = seq_count // 2
    chip = s // 2
    other = s ^ 1
    listed = sources[0]

    query_parts = [lax.dynamic_slice_in_dim(queries, sp_place * head_width, head_width, 1)]
    for d in range(1, sp_count):
        columns = ((sp_place + d) % sp_count) * head_width
        piece = lax.dynamic_slice_in_dim(queries, columns, head_width, 1)
        query_parts.append(
            lax.ppermute(piece, "sp", [(i, (i + d) % sp_count) for i in range(sp_count)])
        )
    order = [0] + sorted(range(1, sp_count), key=lambda d: -min(d, sp_count - d))
    query_block = jnp.concatenate([query_parts[d] for d in order], axis=0)

    back = [(i, (i - 2) % seq_count) for i in range(seq_count)]
    forth = [(i, (i + 2) % seq_count) for i in range(seq_count)]
    t = (s - 2) % seq_count
    t_chip = t // 2
    remote_ids = [seq_count + t, seq_count + (t ^ 1), t, t ^ 1]
    remote_valid = [
        s >= 2,
        s >= 2,
        (t_chip == 0) | (t_chip == chips - 1),
        (t_chip == 0) | (t_chip == chips - 1),
    ]
    if chips > 2:
        remote_ids += [t % 2, 1 - t % 2]
        remote_valid += [(t_chip >= 1) & (t_chip <= chips - 2)] * 2
    remote_flags = membership(listed, remote_ids, remote_valid)
    half = query_block.shape[0] // 2
    got_first, got_flags = lax.ppermute((query_block[:half], remote_flags), "seq", back)
    got_halves = [got_first, lax.ppermute(query_block[half:], "seq", back)]

    swap = [(i, i ^ 1) for i in range(seq_count)]
    partner_k, partner_v, partner_ck, partner_cv = lax.ppermute(
        (new_keys, new_values, cache_keys, cache_values), "seq", swap
    )
    keys = [new_keys, partner_k, cache_keys, partner_ck]
    values = [new_values, partner_v, cache_values, partner_cv]

    if chips > 2:
        first = (cache_keys, cache_values)
        span = 1
        while span < chips - 1:
            pairs = [
                (2 * c + k, 2 * (c + span) + k)
                for c in range(span)
                if c + span < chips - 1
                for k in range(2)
            ]
            got = lax.ppermute(first, "seq", pairs)
            taking = (chip >= span) & (chip < 2 * span)
            first = tuple(jnp.where(taking, b, a) for a, b in zip(first, got))
            span *= 2
        first_other = lax.ppermute(first, "seq", swap)
        remote_keys = keys + [first[0], first_other[0]]
        remote_values = values + [first[1], first_other[1]]
    else:
        remote_keys, remote_values = keys, values

    local_flags = membership(
        listed,
        [seq_count + s, seq_count + other, s, other],
        [s >= 0, s >= 0, chip == 0, chip == 0],
    )
    local_out, local_lse = attend_partial(local_flags, query_block, keys, values, jnp.float32)
    got_first, local_out, local_lse = lax.optimization_barrier((got_halves[0], local_out, local_lse))
    got_halves = [got_first, got_halves[1]]

    mixed_halves = []
    for k, got_query in enumerate(got_halves):
        far_out, far_lse = attend_partial(
            got_flags, got_query, remote_keys, remote_values, jnp.bfloat16
        )
        far_out, far_lse = lax.ppermute((far_out, far_lse), "seq", forth)
        near = slice(k * half, (k + 1) * half)
        lse_a = local_lse[:, 0, near][:, :, None]
        lse_b = far_lse[:, 0, :][:, :, None]
        top = jnp.maximum(lse_a, lse_b)
        weight_a = jnp.exp(lse_a - top)
        weight_b = jnp.exp(lse_b - top)
        mixed = (
            local_out[:, near] * weight_a + far_out.astype(jnp.float32) * weight_b
        ) / (weight_a + weight_b)
        mixed_halves.append(
            jnp.transpose(mixed.astype(jnp.bfloat16), (1, 0, 2)).reshape(half, head_width)
        )

    rows = queries.shape[0]
    result = jnp.zeros((rows, queries.shape[1]), jnp.bfloat16)
    for d in range(sp_count):
        start = order.index(d) * rows
        piece = mixed_halves[start // half][start % half : start % half + rows]
        if d:
            piece = lax.ppermute(piece, "sp", [(i, (i - d) % sp_count) for i in range(sp_count)])
        columns = ((sp_place + d) % sp_count) * head_width
        result = lax.dynamic_update_slice_in_dim(result, piece, columns, 1)
    return result


def solution(mesh):
    return jax.shard_map(
        local,
        mesh=mesh,
        in_specs=(
            P(("groups", "seq", "sp"), None),
            P(("groups", "seq"), "sp"),
            P(("groups", "seq"), "sp"),
            P(("groups", "seq"), "sp"),
            P(("groups", "seq"), "sp"),
            P(("groups", "seq"), None),
        ),
        out_specs=P(("groups", "seq", "sp"), None),
        check_vma=False,
    )
```

```python
import math

import jax
import jax.numpy as jnp
from jax import lax
from jax.experimental import pallas as pl
from jax.experimental.pallas import tpu as pltpu
from jax.sharding import PartitionSpec as P

HEAD_DIM = 128
ROW_SPLIT = 1
STAT_ROWS = 8


def partial_kernel(nsrc, group, flags_ref, q_ref, *refs):
    key_refs = refs[:nsrc]
    value_refs = refs[nsrc : 2 * nsrc]
    out_ref, lse_ref = refs[2 * nsrc : 2 * nsrc + 2]
    score_ref = refs[2 * nsrc + 2]
    score_scale = 1.0 / math.sqrt(HEAD_DIM)
    for g in range(group):
        cols = slice(g * HEAD_DIM, (g + 1) * HEAD_DIM)
        query = q_ref[:, cols]
        top = None
        for j in range(nsrc):
            scores = lax.dot_general(
                query,
                key_refs[j][:, cols],
                (((1,), (1,)), ((), ())),
                preferred_element_type=jnp.float32,
            ) * score_scale
            scores = jnp.where(flags_ref[j] > 0, scores, -1e30)
            score_ref[j] = scores
            block_top = jnp.max(scores, axis=1, keepdims=True)
            top = block_top if top is None else jnp.maximum(top, block_top)
        total = None
        summed = None
        for j in range(nsrc):
            weights = jnp.exp(score_ref[j] - top)
            part_total = jnp.sum(weights, axis=1, keepdims=True)
            product = jnp.dot(
                weights.astype(jnp.bfloat16), value_refs[j][:, cols], preferred_element_type=jnp.float32
            )
            total = part_total if total is None else total + part_total
            summed = product if summed is None else summed + product
        out_ref[g] = (summed / total).astype(out_ref.dtype)
        lse = top + jnp.log(total)
        wide = jnp.broadcast_to(lse, (lse.shape[0], 128))
        lse_ref[g] = jnp.transpose(wide)[:STAT_ROWS]


def attend_partial(flags, query_block, key_blocks, value_blocks, out_dtype):
    nsrc = len(key_blocks)
    rows, width = query_block.shape
    block_rows = key_blocks[0].shape[0]
    nheads = width // HEAD_DIM
    group = max(g for g in range(1, 6) if nheads % g == 0)
    row_tile = rows // ROW_SPLIT
    span = group * HEAD_DIM
    q_spec = pl.BlockSpec((row_tile, span), lambda h, r, f: (r, h))
    kv_spec = pl.BlockSpec((block_rows, span), lambda h, r, f: (0, h))
    out_spec = pl.BlockSpec((group, row_tile, HEAD_DIM), lambda h, r, f: (h, r, 0))
    lse_spec = pl.BlockSpec((group, STAT_ROWS, row_tile), lambda h, r, f: (h, 0, r))
    grid_spec = pltpu.PrefetchScalarGridSpec(
        num_scalar_prefetch=1,
        grid=(nheads // group, ROW_SPLIT),
        in_specs=[q_spec] + [kv_spec] * (2 * nsrc),
        out_specs=[out_spec, lse_spec],
        scratch_shapes=[pltpu.VMEM((nsrc, row_tile, block_rows), jnp.float32)],
    )
    return pl.pallas_call(
        lambda *a: partial_kernel(nsrc, group, *a),
        grid_spec=grid_spec,
        out_shape=[
            jax.ShapeDtypeStruct((nheads, rows, HEAD_DIM), out_dtype),
            jax.ShapeDtypeStruct((nheads, STAT_ROWS, rows), jnp.float32),
        ],
        compiler_params=pltpu.CompilerParams(dimension_semantics=("parallel", "arbitrary")),
    )(flags, query_block, *key_blocks, *value_blocks)


def membership(listed, block_ids, valid):
    hit = jnp.any(listed[None, :] == jnp.stack(block_ids)[:, None], axis=1)
    return (hit & jnp.stack(valid)).astype(jnp.int32)


def local(queries, new_keys, new_values, cache_keys, cache_values, sources):
    head_width = new_keys.shape[1]
    nheads = head_width // HEAD_DIM
    sp_count = lax.axis_size("sp")
    sp_place = lax.axis_index("sp")
    seq_count = lax.axis_size("seq")
    s = lax.axis_index("seq")
    chips = seq_count // 2
    chip = s // 2
    other = s ^ 1
    listed = sources[0]

    query_parts = [lax.dynamic_slice_in_dim(queries, sp_place * head_width, head_width, 1)]
    for d in range(1, sp_count):
        columns = ((sp_place + d) % sp_count) * head_width
        piece = lax.dynamic_slice_in_dim(queries, columns, head_width, 1)
        query_parts.append(
            lax.ppermute(piece, "sp", [(i, (i + d) % sp_count) for i in range(sp_count)])
        )
    query_block = jnp.concatenate(query_parts, axis=0)

    back = [(i, (i - 2) % seq_count) for i in range(seq_count)]
    forth = [(i, (i + 2) % seq_count) for i in range(seq_count)]
    t = (s - 2) % seq_count
    t_chip = t // 2
    remote_ids = [seq_count + t, seq_count + (t ^ 1), t, t ^ 1]
    remote_valid = [
        s >= 2,
        s >= 2,
        (t_chip == 0) | (t_chip == chips - 1),
        (t_chip == 0) | (t_chip == chips - 1),
    ]
    if chips > 2:
        remote_ids += [t % 2, 1 - t % 2]
        remote_valid += [(t_chip >= 1) & (t_chip <= chips - 2)] * 2
    remote_flags = membership(listed, remote_ids, remote_valid)
    half = query_block.shape[0] // 2
    got_flags = lax.ppermute(remote_flags, "seq", back)
    got_halves = [
        lax.ppermute(query_block[:half], "seq", back),
        lax.ppermute(query_block[half:], "seq", back),
    ]

    swap = [(i, i ^ 1) for i in range(seq_count)]
    partner_k, partner_v, partner_ck, partner_cv = lax.ppermute(
        (new_keys, new_values, cache_keys, cache_values), "seq", swap
    )
    keys = [new_keys, partner_k, cache_keys, partner_ck]
    values = [new_values, partner_v, cache_values, partner_cv]

    if chips > 2:
        first = (cache_keys, cache_values)
        span = 1
        while span < chips - 1:
            pairs = [
                (2 * c + k, 2 * (c + span) + k)
                for c in range(span)
                if c + span < chips - 1
                for k in range(2)
            ]
            got = lax.ppermute(first, "seq", pairs)
            taking = (chip >= span) & (chip < 2 * span)
            first = tuple(jnp.where(taking, b, a) for a, b in zip(first, got))
            span *= 2
        first_other = lax.ppermute(first, "seq", swap)
        remote_keys = keys + [first[0], first_other[0]]
        remote_values = values + [first[1], first_other[1]]
    else:
        remote_keys, remote_values = keys, values

    local_flags = membership(
        listed,
        [seq_count + s, seq_count + other, s, other],
        [s >= 0, s >= 0, chip == 0, chip == 0],
    )
    local_out, local_lse = attend_partial(local_flags, query_block, keys, values, jnp.float32)

    mixed_halves = []
    for k, got_query in enumerate(got_halves):
        far_out, far_lse = attend_partial(
            got_flags, got_query, remote_keys, remote_values, jnp.bfloat16
        )
        far_out, far_lse = lax.ppermute((far_out, far_lse), "seq", forth)
        near = slice(k * half, (k + 1) * half)
        lse_a = local_lse[:, 0, near][:, :, None]
        lse_b = far_lse[:, 0, :][:, :, None]
        top = jnp.maximum(lse_a, lse_b)
        weight_a = jnp.exp(lse_a - top)
        weight_b = jnp.exp(lse_b - top)
        mixed = (
            local_out[:, near] * weight_a + far_out.astype(jnp.float32) * weight_b
        ) / (weight_a + weight_b)
        mixed_halves.append(mixed.astype(jnp.bfloat16))
    rows_all = query_block.shape[0]
    heads_out = jnp.transpose(jnp.concatenate(mixed_halves, axis=1), (1, 0, 2)).reshape(
        rows_all, head_width
    )

    rows = queries.shape[0]
    result = jnp.zeros((rows, queries.shape[1]), jnp.bfloat16)
    for d in range(sp_count):
        piece = heads_out[d * rows : (d + 1) * rows]
        if d:
            piece = lax.ppermute(piece, "sp", [(i, (i - d) % sp_count) for i in range(sp_count)])
        columns = ((sp_place + d) % sp_count) * head_width
        result = lax.dynamic_update_slice_in_dim(result, piece, columns, 1)
    return result


def solution(mesh):
    return jax.shard_map(
        local,
        mesh=mesh,
        in_specs=(
            P(("groups", "seq", "sp"), None),
            P(("groups", "seq"), "sp"),
            P(("groups", "seq"), "sp"),
            P(("groups", "seq"), "sp"),
            P(("groups", "seq"), "sp"),
            P(("groups", "seq"), None),
        ),
        out_specs=P(("groups", "seq", "sp"), None),
        check_vma=False,
    )
```

```python
import math

import jax
import jax.numpy as jnp
from jax import lax
from jax.experimental import pallas as pl
from jax.experimental.pallas import tpu as pltpu
from jax.sharding import PartitionSpec as P

HEAD_DIM = 128
ROW_SPLIT = 1
STAT_ROWS = 8


def partial_kernel(nsrc, group, flags_ref, q_ref, *refs):
    key_refs = refs[:nsrc]
    value_refs = refs[nsrc : 2 * nsrc]
    out_ref, lse_ref = refs[2 * nsrc : 2 * nsrc + 2]
    score_ref = refs[2 * nsrc + 2]
    score_scale = 1.0 / math.sqrt(HEAD_DIM)
    for g in range(group):
        cols = slice(g * HEAD_DIM, (g + 1) * HEAD_DIM)
        query = q_ref[:, cols]
        top = None
        for j in range(nsrc):
            scores = lax.dot_general(
                query,
                key_refs[j][:, cols],
                (((1,), (1,)), ((), ())),
                preferred_element_type=jnp.float32,
            ) * score_scale
            scores = jnp.where(flags_ref[j] > 0, scores, -1e30)
            score_ref[j] = scores
            block_top = jnp.max(scores, axis=1, keepdims=True)
            top = block_top if top is None else jnp.maximum(top, block_top)
        total = None
        summed = None
        for j in range(nsrc):
            weights = jnp.exp(score_ref[j] - top)
            part_total = jnp.sum(weights, axis=1, keepdims=True)
            product = jnp.dot(
                weights.astype(jnp.bfloat16), value_refs[j][:, cols], preferred_element_type=jnp.float32
            )
            total = part_total if total is None else total + part_total
            summed = product if summed is None else summed + product
        out_ref[g] = (summed / total).astype(out_ref.dtype)
        lse = top + jnp.log(total)
        wide = jnp.broadcast_to(lse, (lse.shape[0], 128))
        lse_ref[g] = jnp.transpose(wide)[:STAT_ROWS]


def attend_partial(flags, query_block, key_blocks, value_blocks, out_dtype):
    nsrc = len(key_blocks)
    rows, width = query_block.shape
    block_rows = key_blocks[0].shape[0]
    nheads = width // HEAD_DIM
    group = max(g for g in range(1, 6) if nheads % g == 0)
    row_tile = rows // ROW_SPLIT
    span = group * HEAD_DIM
    q_spec = pl.BlockSpec((row_tile, span), lambda h, r, f: (r, h))
    kv_spec = pl.BlockSpec((block_rows, span), lambda h, r, f: (0, h))
    out_spec = pl.BlockSpec((group, row_tile, HEAD_DIM), lambda h, r, f: (h, r, 0))
    lse_spec = pl.BlockSpec((group, STAT_ROWS, row_tile), lambda h, r, f: (h, 0, r))
    grid_spec = pltpu.PrefetchScalarGridSpec(
        num_scalar_prefetch=1,
        grid=(nheads // group, ROW_SPLIT),
        in_specs=[q_spec] + [kv_spec] * (2 * nsrc),
        out_specs=[out_spec, lse_spec],
        scratch_shapes=[pltpu.VMEM((nsrc, row_tile, block_rows), jnp.float32)],
    )
    return pl.pallas_call(
        lambda *a: partial_kernel(nsrc, group, *a),
        grid_spec=grid_spec,
        out_shape=[
            jax.ShapeDtypeStruct((nheads, rows, HEAD_DIM), out_dtype),
            jax.ShapeDtypeStruct((nheads, STAT_ROWS, rows), jnp.float32),
        ],
        compiler_params=pltpu.CompilerParams(dimension_semantics=("parallel", "arbitrary")),
    )(flags, query_block, *key_blocks, *value_blocks)


def membership(listed, block_ids, valid):
    hit = jnp.any(listed[None, :] == jnp.stack(block_ids)[:, None], axis=1)
    return (hit & jnp.stack(valid)).astype(jnp.int32)


def local(queries, new_keys, new_values, cache_keys, cache_values, sources):
    head_width = new_keys.shape[1]
    nheads = head_width // HEAD_DIM
    sp_count = lax.axis_size("sp")
    sp_place = lax.axis_index("sp")
    seq_count = lax.axis_size("seq")
    s = lax.axis_index("seq")
    chips = seq_count // 2
    chip = s // 2
    other = s ^ 1
    listed = sources[0]

    query_parts = [lax.dynamic_slice_in_dim(queries, sp_place * head_width, head_width, 1)]
    for d in range(1, sp_count):
        columns = ((sp_place + d) % sp_count) * head_width
        piece = lax.dynamic_slice_in_dim(queries, columns, head_width, 1)
        query_parts.append(
            lax.ppermute(piece, "sp", [(i, (i + d) % sp_count) for i in range(sp_count)])
        )
    query_block = jnp.concatenate(query_parts, axis=0)

    back = [(i, (i - 2) % seq_count) for i in range(seq_count)]
    forth = [(i, (i + 2) % seq_count) for i in range(seq_count)]
    t = (s - 2) % seq_count
    t_chip = t // 2
    remote_ids = [seq_count + t, seq_count + (t ^ 1), t, t ^ 1]
    remote_valid = [
        s >= 2,
        s >= 2,
        (t_chip == 0) | (t_chip == chips - 1),
        (t_chip == 0) | (t_chip == chips - 1),
    ]
    if chips > 2:
        remote_ids += [t % 2, 1 - t % 2]
        remote_valid += [(t_chip >= 1) & (t_chip <= chips - 2)] * 2
    remote_flags = membership(listed, remote_ids, remote_valid)
    half = query_block.shape[0] // 2
    got_flags = lax.ppermute(remote_flags, "seq", back)
    got_halves = [
        lax.ppermute(query_block[:half], "seq", back),
        lax.ppermute(query_block[half:], "seq", back),
    ]

    swap = [(i, i ^ 1) for i in range(seq_count)]
    partner_k, partner_v, partner_ck, partner_cv = lax.ppermute(
        (new_keys, new_values, cache_keys, cache_values), "seq", swap
    )
    keys = [new_keys, partner_k, cache_keys, partner_ck]
    values = [new_values, partner_v, cache_values, partner_cv]

    if chips > 2:
        first = (cache_keys, cache_values)
        span = 1
        while span < chips - 1:
            pairs = [
                (2 * c + k, 2 * (c + span) + k)
                for c in range(span)
                if c + span < chips - 1
                for k in range(2)
            ]
            got = lax.ppermute(first, "seq", pairs)
            taking = (chip >= span) & (chip < 2 * span)
            first = tuple(jnp.where(taking, b, a) for a, b in zip(first, got))
            span *= 2
        first_other = lax.ppermute(first, "seq", swap)
        remote_keys = keys + [first[0], first_other[0]]
        remote_values = values + [first[1], first_other[1]]
    else:
        remote_keys, remote_values = keys, values

    local_flags = membership(
        listed,
        [seq_count + s, seq_count + other, s, other],
        [s >= 0, s >= 0, chip == 0, chip == 0],
    )
    local_out, local_lse = attend_partial(local_flags, query_block, keys, values, jnp.float32)
    got_first, local_out, local_lse = lax.optimization_barrier((got_halves[0], local_out, local_lse))
    got_halves = [got_first, got_halves[1]]

    mixed_halves = []
    for k, got_query in enumerate(got_halves):
        far_out, far_lse = attend_partial(
            got_flags, got_query, remote_keys, remote_values, jnp.bfloat16
        )
        far_out, far_lse = lax.ppermute((far_out, far_lse), "seq", forth)
        near = slice(k * half, (k + 1) * half)
        lse_a = local_lse[:, 0, near][:, :, None]
        lse_b = far_lse[:, 0, :][:, :, None]
        top = jnp.maximum(lse_a, lse_b)
        weight_a = jnp.exp(lse_a - top)
        weight_b = jnp.exp(lse_b - top)
        mixed = (
            local_out[:, near] * weight_a + far_out.astype(jnp.float32) * weight_b
        ) / (weight_a + weight_b)
        mixed_halves.append(mixed.astype(jnp.bfloat16))
    rows_all = query_block.shape[0]
    heads_out = jnp.transpose(jnp.concatenate(mixed_halves, axis=1), (1, 0, 2)).reshape(
        rows_all, head_width
    )

    rows = queries.shape[0]
    result = jnp.zeros((rows, queries.shape[1]), jnp.bfloat16)
    for d in range(sp_count):
        piece = heads_out[d * rows : (d + 1) * rows]
        if d:
            piece = lax.ppermute(piece, "sp", [(i, (i - d) % sp_count) for i in range(sp_count)])
        columns = ((sp_place + d) % sp_count) * head_width
        result = lax.dynamic_update_slice_in_dim(result, piece, columns, 1)
    return result


def solution(mesh):
    return jax.shard_map(
        local,
        mesh=mesh,
        in_specs=(
            P(("groups", "seq", "sp"), None),
            P(("groups", "seq"), "sp"),
            P(("groups", "seq"), "sp"),
            P(("groups", "seq"), "sp"),
            P(("groups", "seq"), "sp"),
            P(("groups", "seq"), None),
        ),
        out_specs=P(("groups", "seq", "sp"), None),
        check_vma=False,
    )
```

```python
import math

import jax
import jax.numpy as jnp
from jax import lax
from jax.experimental import pallas as pl
from jax.experimental.pallas import tpu as pltpu
from jax.sharding import PartitionSpec as P

HEAD_DIM = 128
ROW_SPLIT = 1
STAT_ROWS = 8


def partial_kernel(nsrc, group, flags_ref, q_ref, *refs):
    key_refs = refs[:nsrc]
    value_refs = refs[nsrc : 2 * nsrc]
    out_ref, lse_ref = refs[2 * nsrc : 2 * nsrc + 2]
    score_ref = refs[2 * nsrc + 2]
    score_scale = 1.0 / math.sqrt(HEAD_DIM)
    for g in range(group):
        cols = slice(g * HEAD_DIM, (g + 1) * HEAD_DIM)
        query = q_ref[:, cols]
        top = None
        for j in range(nsrc):
            scores = lax.dot_general(
                query,
                key_refs[j][:, cols],
                (((1,), (1,)), ((), ())),
                preferred_element_type=jnp.float32,
            ) * score_scale
            scores = jnp.where(flags_ref[j] > 0, scores, -1e30)
            score_ref[j] = scores
            block_top = jnp.max(scores, axis=1, keepdims=True)
            top = block_top if top is None else jnp.maximum(top, block_top)
        total = None
        summed = None
        for j in range(nsrc):
            weights = jnp.exp(score_ref[j] - top)
            part_total = jnp.sum(weights, axis=1, keepdims=True)
            product = jnp.dot(
                weights.astype(jnp.bfloat16), value_refs[j][:, cols], preferred_element_type=jnp.float32
            )
            total = part_total if total is None else total + part_total
            summed = product if summed is None else summed + product
        out_ref[g] = (summed / total).astype(out_ref.dtype)
        lse = top + jnp.log(total)
        wide = jnp.broadcast_to(lse, (lse.shape[0], 128))
        lse_ref[g] = jnp.transpose(wide)[:STAT_ROWS]


def attend_partial(flags, query_block, key_blocks, value_blocks, out_dtype):
    nsrc = len(key_blocks)
    rows, width = query_block.shape
    block_rows = key_blocks[0].shape[0]
    nheads = width // HEAD_DIM
    group = max(g for g in range(1, 6) if nheads % g == 0)
    row_tile = rows // ROW_SPLIT
    span = group * HEAD_DIM
    q_spec = pl.BlockSpec((row_tile, span), lambda h, r, f: (r, h))
    kv_spec = pl.BlockSpec((block_rows, span), lambda h, r, f: (0, h))
    out_spec = pl.BlockSpec((group, row_tile, HEAD_DIM), lambda h, r, f: (h, r, 0))
    lse_spec = pl.BlockSpec((group, STAT_ROWS, row_tile), lambda h, r, f: (h, 0, r))
    grid_spec = pltpu.PrefetchScalarGridSpec(
        num_scalar_prefetch=1,
        grid=(nheads // group, ROW_SPLIT),
        in_specs=[q_spec] + [kv_spec] * (2 * nsrc),
        out_specs=[out_spec, lse_spec],
        scratch_shapes=[pltpu.VMEM((nsrc, row_tile, block_rows), jnp.float32)],
    )
    return pl.pallas_call(
        lambda *a: partial_kernel(nsrc, group, *a),
        grid_spec=grid_spec,
        out_shape=[
            jax.ShapeDtypeStruct((nheads, rows, HEAD_DIM), out_dtype),
            jax.ShapeDtypeStruct((nheads, STAT_ROWS, rows), jnp.float32),
        ],
        compiler_params=pltpu.CompilerParams(dimension_semantics=("parallel", "arbitrary")),
    )(flags, query_block, *key_blocks, *value_blocks)


def membership(listed, block_ids, valid):
    hit = jnp.any(listed[None, :] == jnp.stack(block_ids)[:, None], axis=1)
    return (hit & jnp.stack(valid)).astype(jnp.int32)


def local(queries, new_keys, new_values, cache_keys, cache_values, sources):
    head_width = new_keys.shape[1]
    nheads = head_width // HEAD_DIM
    sp_count = lax.axis_size("sp")
    sp_place = lax.axis_index("sp")
    seq_count = lax.axis_size("seq")
    s = lax.axis_index("seq")
    chips = seq_count // 2
    chip = s // 2
    other = s ^ 1
    listed = sources[0]

    query_parts = [lax.dynamic_slice_in_dim(queries, sp_place * head_width, head_width, 1)]
    for d in range(1, sp_count):
        columns = ((sp_place + d) % sp_count) * head_width
        piece = lax.dynamic_slice_in_dim(queries, columns, head_width, 1)
        query_parts.append(
            lax.ppermute(piece, "sp", [(i, (i + d) % sp_count) for i in range(sp_count)])
        )
    query_block = jnp.concatenate(query_parts, axis=0)

    back = [(i, (i - 2) % seq_count) for i in range(seq_count)]
    forth = [(i, (i + 2) % seq_count) for i in range(seq_count)]
    t = (s - 2) % seq_count
    t_chip = t // 2
    remote_ids = [seq_count + t, seq_count + (t ^ 1), t, t ^ 1]
    remote_valid = [
        s >= 2,
        s >= 2,
        (t_chip == 0) | (t_chip == chips - 1),
        (t_chip == 0) | (t_chip == chips - 1),
    ]
    if chips > 2:
        remote_ids += [t % 2, 1 - t % 2]
        remote_valid += [(t_chip >= 1) & (t_chip <= chips - 2)] * 2
    remote_flags = membership(listed, remote_ids, remote_valid)
    half = query_block.shape[0] // 2
    got_flags = lax.ppermute(remote_flags, "seq", back)
    got_halves = [
        lax.ppermute(query_block[:half], "seq", back),
        lax.ppermute(query_block[half:], "seq", back),
    ]

    swap = [(i, i ^ 1) for i in range(seq_count)]
    partner_k, partner_v, partner_ck, partner_cv = lax.ppermute(
        (new_keys, new_values, cache_keys, cache_values), "seq", swap
    )
    keys = [new_keys, partner_k, cache_keys, partner_ck]
    values = [new_values, partner_v, cache_values, partner_cv]

    if chips > 2:
        first = (cache_keys, cache_values)
        span = 1
        while span < chips - 1:
            pairs = [
                (2 * c + k, 2 * (c + span) + k)
                for c in range(span)
                if c + span < chips - 1
                for k in range(2)
            ]
            got = lax.ppermute(first, "seq", pairs)
            taking = (chip >= span) & (chip < 2 * span)
            first = tuple(jnp.where(taking, b, a) for a, b in zip(first, got))
            span *= 2
        first_other = lax.ppermute(first, "seq", swap)
        remote_keys = keys + [first[0], first_other[0]]
        remote_values = values + [first[1], first_other[1]]
    else:
        remote_keys, remote_values = keys, values

    local_flags = membership(
        listed,
        [seq_count + s, seq_count + other, s, other],
        [s >= 0, s >= 0, chip == 0, chip == 0],
    )
    local_out, local_lse = attend_partial(local_flags, query_block, keys, values, jnp.float32)

    mixed_halves = []
    for k, got_query in enumerate(got_halves):
        far_out, far_lse = attend_partial(
            got_flags, got_query, remote_keys, remote_values, jnp.bfloat16
        )
        far_out, far_lse = lax.ppermute((far_out, far_lse), "seq", forth)
        near = slice(k * half, (k + 1) * half)
        lse_a = local_lse[:, 0, near][:, :, None]
        lse_b = far_lse[:, 0, :][:, :, None]
        top = jnp.maximum(lse_a, lse_b)
        weight_a = jnp.exp(lse_a - top)
        weight_b = jnp.exp(lse_b - top)
        mixed = (
            local_out[:, near] * weight_a + far_out.astype(jnp.float32) * weight_b
        ) / (weight_a + weight_b)
        mixed_halves.append(mixed.astype(jnp.bfloat16))

    rows = queries.shape[0]
    result = jnp.zeros((rows, queries.shape[1]), jnp.bfloat16)
    for d in range(sp_count):
        start = d * rows
        piece = mixed_halves[start // half][:, start % half : start % half + rows]
        if d:
            piece = lax.ppermute(piece, "sp", [(i, (i - d) % sp_count) for i in range(sp_count)])
        piece = jnp.transpose(piece, (1, 0, 2)).reshape(rows, head_width)
        columns = ((sp_place + d) % sp_count) * head_width
        result = lax.dynamic_update_slice_in_dim(result, piece, columns, 1)
    return result


def solution(mesh):
    return jax.shard_map(
        local,
        mesh=mesh,
        in_specs=(
            P(("groups", "seq", "sp"), None),
            P(("groups", "seq"), "sp"),
            P(("groups", "seq"), "sp"),
            P(("groups", "seq"), "sp"),
            P(("groups", "seq"), "sp"),
            P(("groups", "seq"), None),
        ),
        out_specs=P(("groups", "seq", "sp"), None),
        check_vma=False,
    )
```

```python
import math

import jax
import jax.numpy as jnp
from jax import lax
from jax.experimental import pallas as pl
from jax.experimental.pallas import tpu as pltpu
from jax.sharding import PartitionSpec as P

HEAD_DIM = 128
ROW_SPLIT = 1
STAT_ROWS = 8


def partial_kernel(nsrc, group, flags_ref, q_ref, *refs):
    key_refs = refs[:nsrc]
    value_refs = refs[nsrc : 2 * nsrc]
    out_ref, lse_ref = refs[2 * nsrc : 2 * nsrc + 2]
    score_ref = refs[2 * nsrc + 2]
    score_scale = 1.0 / math.sqrt(HEAD_DIM)
    for g in range(group):
        cols = slice(g * HEAD_DIM, (g + 1) * HEAD_DIM)
        query = q_ref[:, cols]
        top = None
        for j in range(nsrc):
            scores = lax.dot_general(
                query,
                key_refs[j][:, cols],
                (((1,), (1,)), ((), ())),
                preferred_element_type=jnp.float32,
            ) * score_scale
            scores = jnp.where(flags_ref[j] > 0, scores, -1e30)
            score_ref[j] = scores
            block_top = jnp.max(scores, axis=1, keepdims=True)
            top = block_top if top is None else jnp.maximum(top, block_top)
        total = None
        summed = None
        for j in range(nsrc):
            weights = jnp.exp(score_ref[j] - top)
            part_total = jnp.sum(weights, axis=1, keepdims=True)
            product = jnp.dot(
                weights.astype(jnp.bfloat16), value_refs[j][:, cols], preferred_element_type=jnp.float32
            )
            total = part_total if total is None else total + part_total
            summed = product if summed is None else summed + product
        out_ref[g] = (summed / total).astype(out_ref.dtype)
        lse = top + jnp.log(total)
        wide = jnp.broadcast_to(lse, (lse.shape[0], 128))
        lse_ref[g] = jnp.transpose(wide)[:STAT_ROWS]


def attend_partial(flags, query_block, key_blocks, value_blocks, out_dtype):
    nsrc = len(key_blocks)
    rows, width = query_block.shape
    block_rows = key_blocks[0].shape[0]
    nheads = width // HEAD_DIM
    group = max(g for g in range(1, 6) if nheads % g == 0)
    row_tile = rows // ROW_SPLIT
    span = group * HEAD_DIM
    q_spec = pl.BlockSpec((row_tile, span), lambda h, r, f: (r, h))
    kv_spec = pl.BlockSpec((block_rows, span), lambda h, r, f: (0, h))
    out_spec = pl.BlockSpec((group, row_tile, HEAD_DIM), lambda h, r, f: (h, r, 0))
    lse_spec = pl.BlockSpec((group, STAT_ROWS, row_tile), lambda h, r, f: (h, 0, r))
    grid_spec = pltpu.PrefetchScalarGridSpec(
        num_scalar_prefetch=1,
        grid=(nheads // group, ROW_SPLIT),
        in_specs=[q_spec] + [kv_spec] * (2 * nsrc),
        out_specs=[out_spec, lse_spec],
        scratch_shapes=[pltpu.VMEM((nsrc, row_tile, block_rows), jnp.float32)],
    )
    return pl.pallas_call(
        lambda *a: partial_kernel(nsrc, group, *a),
        grid_spec=grid_spec,
        out_shape=[
            jax.ShapeDtypeStruct((nheads, rows, HEAD_DIM), out_dtype),
            jax.ShapeDtypeStruct((nheads, STAT_ROWS, rows), jnp.float32),
        ],
        compiler_params=pltpu.CompilerParams(dimension_semantics=("parallel", "arbitrary")),
    )(flags, query_block, *key_blocks, *value_blocks)


def membership(listed, block_ids, valid):
    hit = jnp.any(listed[None, :] == jnp.stack(block_ids)[:, None], axis=1)
    return (hit & jnp.stack(valid)).astype(jnp.int32)


def local(queries, new_keys, new_values, cache_keys, cache_values, sources):
    head_width = new_keys.shape[1]
    nheads = head_width // HEAD_DIM
    sp_count = lax.axis_size("sp")
    sp_place = lax.axis_index("sp")
    seq_count = lax.axis_size("seq")
    s = lax.axis_index("seq")
    chips = seq_count // 2
    chip = s // 2
    other = s ^ 1
    listed = sources[0]

    query_parts = [lax.dynamic_slice_in_dim(queries, sp_place * head_width, head_width, 1)]
    for d in range(1, sp_count):
        columns = ((sp_place + d) % sp_count) * head_width
        piece = lax.dynamic_slice_in_dim(queries, columns, head_width, 1)
        query_parts.append(
            lax.ppermute(piece, "sp", [(i, (i + d) % sp_count) for i in range(sp_count)])
        )
    query_block = jnp.concatenate(query_parts, axis=0)

    back = [(i, (i - 2) % seq_count) for i in range(seq_count)]
    forth = [(i, (i + 2) % seq_count) for i in range(seq_count)]
    t = (s - 2) % seq_count
    t_chip = t // 2
    remote_ids = [seq_count + t, seq_count + (t ^ 1), t, t ^ 1]
    remote_valid = [
        s >= 2,
        s >= 2,
        (t_chip == 0) | (t_chip == chips - 1),
        (t_chip == 0) | (t_chip == chips - 1),
    ]
    if chips > 2:
        remote_ids += [t % 2, 1 - t % 2]
        remote_valid += [(t_chip >= 1) & (t_chip <= chips - 2)] * 2
    remote_flags = membership(listed, remote_ids, remote_valid)
    half = query_block.shape[0] // 2
    got_flags = lax.ppermute(remote_flags, "seq", back)
    got_halves = [
        lax.ppermute(query_block[:half], "seq", back),
        lax.ppermute(query_block[half:], "seq", back),
    ]

    swap = [(i, i ^ 1) for i in range(seq_count)]
    partner_k, partner_v, partner_ck, partner_cv = lax.ppermute(
        (new_keys, new_values, cache_keys, cache_values), "seq", swap
    )
    keys = [new_keys, partner_k, cache_keys, partner_ck]
    values = [new_values, partner_v, cache_values, partner_cv]

    if chips > 2:
        first = (cache_keys, cache_values)
        span = 1
        while span < chips - 1:
            pairs = [
                (2 * c + k, 2 * (c + span) + k)
                for c in range(span)
                if c + span < chips - 1
                for k in range(2)
            ]
            got = lax.ppermute(first, "seq", pairs)
            taking = (chip >= span) & (chip < 2 * span)
            first = tuple(jnp.where(taking, b, a) for a, b in zip(first, got))
            span *= 2
        first_other = lax.ppermute(first, "seq", swap)
        remote_keys = keys + [first[0], first_other[0]]
        remote_values = values + [first[1], first_other[1]]
    else:
        remote_keys, remote_values = keys, values

    local_flags = membership(
        listed,
        [seq_count + s, seq_count + other, s, other],
        [s >= 0, s >= 0, chip == 0, chip == 0],
    )
    local_out, local_lse = attend_partial(local_flags, query_block, keys, values, jnp.float32)

    mixed_halves = []
    for k, got_query in enumerate(got_halves):
        far_out, far_lse = attend_partial(
            got_flags, got_query, remote_keys, remote_values, jnp.bfloat16
        )
        far_out, far_lse = lax.ppermute((far_out, far_lse[:, 0, :]), "seq", forth)
        near = slice(k * half, (k + 1) * half)
        lse_a = local_lse[:, 0, near][:, :, None]
        lse_b = far_lse[:, :, None]
        top = jnp.maximum(lse_a, lse_b)
        weight_a = jnp.exp(lse_a - top)
        weight_b = jnp.exp(lse_b - top)
        mixed = (
            local_out[:, near] * weight_a + far_out.astype(jnp.float32) * weight_b
        ) / (weight_a + weight_b)
        mixed_halves.append(mixed.astype(jnp.bfloat16))

    rows = queries.shape[0]
    result = jnp.zeros((rows, queries.shape[1]), jnp.bfloat16)
    for d in range(sp_count):
        start = d * rows
        piece = mixed_halves[start // half][:, start % half : start % half + rows]
        if d:
            piece = lax.ppermute(piece, "sp", [(i, (i - d) % sp_count) for i in range(sp_count)])
        piece = jnp.transpose(piece, (1, 0, 2)).reshape(rows, head_width)
        columns = ((sp_place + d) % sp_count) * head_width
        result = lax.dynamic_update_slice_in_dim(result, piece, columns, 1)
    return result


def solution(mesh):
    return jax.shard_map(
        local,
        mesh=mesh,
        in_specs=(
            P(("groups", "seq", "sp"), None),
            P(("groups", "seq"), "sp"),
            P(("groups", "seq"), "sp"),
            P(("groups", "seq"), "sp"),
            P(("groups", "seq"), "sp"),
            P(("groups", "seq"), None),
        ),
        out_specs=P(("groups", "seq", "sp"), None),
        check_vma=False,
    )
```

```python
import math

import jax
import jax.numpy as jnp
from jax import lax
from jax.experimental import pallas as pl
from jax.experimental.pallas import tpu as pltpu
from jax.sharding import PartitionSpec as P

HEAD_DIM = 128
ROW_SPLIT = 1
STAT_ROWS = 8


def partial_kernel(nsrc, group, flags_ref, q_ref, *refs):
    key_refs = refs[:nsrc]
    value_refs = refs[nsrc : 2 * nsrc]
    out_ref, lse_ref = refs[2 * nsrc : 2 * nsrc + 2]
    score_ref = refs[2 * nsrc + 2]
    score_scale = 1.0 / math.sqrt(HEAD_DIM)
    for g in range(group):
        cols = slice(g * HEAD_DIM, (g + 1) * HEAD_DIM)
        query = q_ref[:, cols]
        top = None
        for j in range(nsrc):
            scores = lax.dot_general(
                query,
                key_refs[j][:, cols],
                (((1,), (1,)), ((), ())),
                preferred_element_type=jnp.float32,
            ) * score_scale
            scores = jnp.where(flags_ref[j] > 0, scores, -1e30)
            score_ref[j] = scores
            block_top = jnp.max(scores, axis=1, keepdims=True)
            top = block_top if top is None else jnp.maximum(top, block_top)
        total = None
        summed = None
        for j in range(nsrc):
            weights = jnp.exp(score_ref[j] - top)
            part_total = jnp.sum(weights, axis=1, keepdims=True)
            product = jnp.dot(
                weights.astype(jnp.bfloat16), value_refs[j][:, cols], preferred_element_type=jnp.float32
            )
            total = part_total if total is None else total + part_total
            summed = product if summed is None else summed + product
        out_ref[g] = (summed / total).astype(out_ref.dtype)
        lse = top + jnp.log(total)
        wide = jnp.broadcast_to(lse, (lse.shape[0], 128))
        lse_ref[g] = jnp.transpose(wide)[:STAT_ROWS]


def attend_partial(flags, query_block, key_blocks, value_blocks, out_dtype):
    nsrc = len(key_blocks)
    rows, width = query_block.shape
    block_rows = key_blocks[0].shape[0]
    nheads = width // HEAD_DIM
    group = max(g for g in range(1, 11) if nheads % g == 0)
    row_tile = rows // ROW_SPLIT
    span = group * HEAD_DIM
    q_spec = pl.BlockSpec((row_tile, span), lambda h, r, f: (r, h))
    kv_spec = pl.BlockSpec((block_rows, span), lambda h, r, f: (0, h))
    out_spec = pl.BlockSpec((group, row_tile, HEAD_DIM), lambda h, r, f: (h, r, 0))
    lse_spec = pl.BlockSpec((group, STAT_ROWS, row_tile), lambda h, r, f: (h, 0, r))
    grid_spec = pltpu.PrefetchScalarGridSpec(
        num_scalar_prefetch=1,
        grid=(nheads // group, ROW_SPLIT),
        in_specs=[q_spec] + [kv_spec] * (2 * nsrc),
        out_specs=[out_spec, lse_spec],
        scratch_shapes=[pltpu.VMEM((nsrc, row_tile, block_rows), jnp.float32)],
    )
    return pl.pallas_call(
        lambda *a: partial_kernel(nsrc, group, *a),
        grid_spec=grid_spec,
        out_shape=[
            jax.ShapeDtypeStruct((nheads, rows, HEAD_DIM), out_dtype),
            jax.ShapeDtypeStruct((nheads, STAT_ROWS, rows), jnp.float32),
        ],
        compiler_params=pltpu.CompilerParams(dimension_semantics=("parallel", "arbitrary")),
    )(flags, query_block, *key_blocks, *value_blocks)


def membership(listed, block_ids, valid):
    hit = jnp.any(listed[None, :] == jnp.stack(block_ids)[:, None], axis=1)
    return (hit & jnp.stack(valid)).astype(jnp.int32)


def local(queries, new_keys, new_values, cache_keys, cache_values, sources):
    head_width = new_keys.shape[1]
    nheads = head_width // HEAD_DIM
    sp_count = lax.axis_size("sp")
    sp_place = lax.axis_index("sp")
    seq_count = lax.axis_size("seq")
    s = lax.axis_index("seq")
    chips = seq_count // 2
    chip = s // 2
    other = s ^ 1
    listed = sources[0]

    query_parts = [lax.dynamic_slice_in_dim(queries, sp_place * head_width, head_width, 1)]
    for d in range(1, sp_count):
        columns = ((sp_place + d) % sp_count) * head_width
        piece = lax.dynamic_slice_in_dim(queries, columns, head_width, 1)
        query_parts.append(
            lax.ppermute(piece, "sp", [(i, (i + d) % sp_count) for i in range(sp_count)])
        )
    query_block = jnp.concatenate(query_parts, axis=0)

    back = [(i, (i - 2) % seq_count) for i in range(seq_count)]
    forth = [(i, (i + 2) % seq_count) for i in range(seq_count)]
    t = (s - 2) % seq_count
    t_chip = t // 2
    remote_ids = [seq_count + t, seq_count + (t ^ 1), t, t ^ 1]
    remote_valid = [
        s >= 2,
        s >= 2,
        (t_chip == 0) | (t_chip == chips - 1),
        (t_chip == 0) | (t_chip == chips - 1),
    ]
    if chips > 2:
        remote_ids += [t % 2, 1 - t % 2]
        remote_valid += [(t_chip >= 1) & (t_chip <= chips - 2)] * 2
    remote_flags = membership(listed, remote_ids, remote_valid)
    half = query_block.shape[0] // 2
    got_flags = lax.ppermute(remote_flags, "seq", back)
    got_halves = [
        lax.ppermute(query_block[:half], "seq", back),
        lax.ppermute(query_block[half:], "seq", back),
    ]

    swap = [(i, i ^ 1) for i in range(seq_count)]
    partner_k, partner_v, partner_ck, partner_cv = lax.ppermute(
        (new_keys, new_values, cache_keys, cache_values), "seq", swap
    )
    keys = [new_keys, partner_k, cache_keys, partner_ck]
    values = [new_values, partner_v, cache_values, partner_cv]

    if chips > 2:
        first = (cache_keys, cache_values)
        span = 1
        while span < chips - 1:
            pairs = [
                (2 * c + k, 2 * (c + span) + k)
                for c in range(span)
                if c + span < chips - 1
                for k in range(2)
            ]
            got = lax.ppermute(first, "seq", pairs)
            taking = (chip >= span) & (chip < 2 * span)
            first = tuple(jnp.where(taking, b, a) for a, b in zip(first, got))
            span *= 2
        first_other = lax.ppermute(first, "seq", swap)
        remote_keys = keys + [first[0], first_other[0]]
        remote_values = values + [first[1], first_other[1]]
    else:
        remote_keys, remote_values = keys, values

    local_flags = membership(
        listed,
        [seq_count + s, seq_count + other, s, other],
        [s >= 0, s >= 0, chip == 0, chip == 0],
    )
    local_out, local_lse = attend_partial(local_flags, query_block, keys, values, jnp.float32)

    mixed_halves = []
    for k, got_query in enumerate(got_halves):
        far_out, far_lse = attend_partial(
            got_flags, got_query, remote_keys, remote_values, jnp.bfloat16
        )
        far_out, far_lse = lax.ppermute((far_out, far_lse), "seq", forth)
        near = slice(k * half, (k + 1) * half)
        lse_a = local_lse[:, 0, near][:, :, None]
        lse_b = far_lse[:, 0, :][:, :, None]
        top = jnp.maximum(lse_a, lse_b)
        weight_a = jnp.exp(lse_a - top)
        weight_b = jnp.exp(lse_b - top)
        mixed = (
            local_out[:, near] * weight_a + far_out.astype(jnp.float32) * weight_b
        ) / (weight_a + weight_b)
        mixed_halves.append(mixed.astype(jnp.bfloat16))

    rows = queries.shape[0]
    result = jnp.zeros((rows, queries.shape[1]), jnp.bfloat16)
    for d in range(sp_count):
        start = d * rows
        piece = mixed_halves[start // half][:, start % half : start % half + rows]
        if d:
            piece = lax.ppermute(piece, "sp", [(i, (i - d) % sp_count) for i in range(sp_count)])
        piece = jnp.transpose(piece, (1, 0, 2)).reshape(rows, head_width)
        columns = ((sp_place + d) % sp_count) * head_width
        result = lax.dynamic_update_slice_in_dim(result, piece, columns, 1)
    return result


def solution(mesh):
    return jax.shard_map(
        local,
        mesh=mesh,
        in_specs=(
            P(("groups", "seq", "sp"), None),
            P(("groups", "seq"), "sp"),
            P(("groups", "seq"), "sp"),
            P(("groups", "seq"), "sp"),
            P(("groups", "seq"), "sp"),
            P(("groups", "seq"), None),
        ),
        out_specs=P(("groups", "seq", "sp"), None),
        check_vma=False,
    )
```

```python
import math

import jax
import jax.numpy as jnp
from jax import lax
from jax.experimental import pallas as pl
from jax.experimental.pallas import tpu as pltpu
from jax.sharding import PartitionSpec as P

HEAD_DIM = 128
ROW_SPLIT = 1
STAT_ROWS = 8


def partial_kernel(nsrc, group, flags_ref, q_ref, *refs):
    key_refs = refs[:nsrc]
    value_refs = refs[nsrc : 2 * nsrc]
    out_ref, lse_ref = refs[2 * nsrc : 2 * nsrc + 2]
    score_ref = refs[2 * nsrc + 2]
    score_scale = 1.0 / math.sqrt(HEAD_DIM)
    for g in range(group):
        cols = slice(g * HEAD_DIM, (g + 1) * HEAD_DIM)
        query = q_ref[:, cols]
        top = None
        for j in range(nsrc):
            scores = lax.dot_general(
                query,
                key_refs[j][:, cols],
                (((1,), (1,)), ((), ())),
                preferred_element_type=jnp.float32,
            ) * score_scale
            scores = jnp.where(flags_ref[j] > 0, scores, -1e30)
            score_ref[j] = scores
            block_top = jnp.max(scores, axis=1, keepdims=True)
            top = block_top if top is None else jnp.maximum(top, block_top)
        total = None
        summed = None
        for j in range(nsrc):
            weights = jnp.exp(score_ref[j] - top)
            part_total = jnp.sum(weights, axis=1, keepdims=True)
            product = jnp.dot(
                weights.astype(jnp.bfloat16), value_refs[j][:, cols], preferred_element_type=jnp.float32
            )
            total = part_total if total is None else total + part_total
            summed = product if summed is None else summed + product
        out_ref[g] = (summed / total).astype(out_ref.dtype)
        lse = top + jnp.log(total)
        wide = jnp.broadcast_to(lse, (lse.shape[0], 128))
        lse_ref[g] = jnp.transpose(wide)[:STAT_ROWS]


def attend_partial(flags, query_block, key_blocks, value_blocks, out_dtype):
    nsrc = len(key_blocks)
    rows, width = query_block.shape
    block_rows = key_blocks[0].shape[0]
    nheads = width // HEAD_DIM
    group = max(g for g in range(1, 6) if nheads % g == 0)
    row_tile = rows // ROW_SPLIT
    span = group * HEAD_DIM
    q_spec = pl.BlockSpec((row_tile, span), lambda h, r, f: (r, h))
    kv_spec = pl.BlockSpec((block_rows, span), lambda h, r, f: (0, h))
    out_spec = pl.BlockSpec((group, row_tile, HEAD_DIM), lambda h, r, f: (h, r, 0))
    lse_spec = pl.BlockSpec((group, STAT_ROWS, row_tile), lambda h, r, f: (h, 0, r))
    grid_spec = pltpu.PrefetchScalarGridSpec(
        num_scalar_prefetch=1,
        grid=(nheads // group, ROW_SPLIT),
        in_specs=[q_spec] + [kv_spec] * (2 * nsrc),
        out_specs=[out_spec, lse_spec],
        scratch_shapes=[pltpu.VMEM((nsrc, row_tile, block_rows), jnp.float32)],
    )
    return pl.pallas_call(
        lambda *a: partial_kernel(nsrc, group, *a),
        grid_spec=grid_spec,
        out_shape=[
            jax.ShapeDtypeStruct((nheads, rows, HEAD_DIM), out_dtype),
            jax.ShapeDtypeStruct((nheads, STAT_ROWS, rows), jnp.float32),
        ],
        compiler_params=pltpu.CompilerParams(dimension_semantics=("parallel", "arbitrary")),
    )(flags, query_block, *key_blocks, *value_blocks)


def membership(listed, block_ids, valid):
    hit = jnp.any(listed[None, :] == jnp.stack(block_ids)[:, None], axis=1)
    return (hit & jnp.stack(valid)).astype(jnp.int32)


def local(queries, new_keys, new_values, cache_keys, cache_values, sources):
    head_width = new_keys.shape[1]
    nheads = head_width // HEAD_DIM
    sp_count = lax.axis_size("sp")
    sp_place = lax.axis_index("sp")
    seq_count = lax.axis_size("seq")
    s = lax.axis_index("seq")
    chips = seq_count // 2
    chip = s // 2
    other = s ^ 1
    listed = sources[0]

    issue = sorted(range(1, sp_count), key=lambda d: -min(d, sp_count - d))
    received = {}
    for d in issue:
        columns = ((sp_place + d) % sp_count) * head_width
        piece = lax.dynamic_slice_in_dim(queries, columns, head_width, 1)
        received[d] = lax.ppermute(piece, "sp", [(i, (i + d) % sp_count) for i in range(sp_count)])
    query_parts = [lax.dynamic_slice_in_dim(queries, sp_place * head_width, head_width, 1)]
    query_parts += [received[d] for d in range(1, sp_count)]
    query_block = jnp.concatenate(query_parts, axis=0)

    back = [(i, (i - 2) % seq_count) for i in range(seq_count)]
    forth = [(i, (i + 2) % seq_count) for i in range(seq_count)]
    t = (s - 2) % seq_count
    t_chip = t // 2
    remote_ids = [seq_count + t, seq_count + (t ^ 1), t, t ^ 1]
    remote_valid = [
        s >= 2,
        s >= 2,
        (t_chip == 0) | (t_chip == chips - 1),
        (t_chip == 0) | (t_chip == chips - 1),
    ]
    if chips > 2:
        remote_ids += [t % 2, 1 - t % 2]
        remote_valid += [(t_chip >= 1) & (t_chip <= chips - 2)] * 2
    remote_flags = membership(listed, remote_ids, remote_valid)
    half = query_block.shape[0] // 2
    got_flags = lax.ppermute(remote_flags, "seq", back)
    got_halves = [
        lax.ppermute(query_block[:half], "seq", back),
        lax.ppermute(query_block[half:], "seq", back),
    ]

    swap = [(i, i ^ 1) for i in range(seq_count)]
    partner_k, partner_v, partner_ck, partner_cv = lax.ppermute(
        (new_keys, new_values, cache_keys, cache_values), "seq", swap
    )
    keys = [new_keys, partner_k, cache_keys, partner_ck]
    values = [new_values, partner_v, cache_values, partner_cv]

    if chips > 2:
        first = (cache_keys, cache_values)
        span = 1
        while span < chips - 1:
            pairs = [
                (2 * c + k, 2 * (c + span) + k)
                for c in range(span)
                if c + span < chips - 1
                for k in range(2)
            ]
            got = lax.ppermute(first, "seq", pairs)
            taking = (chip >= span) & (chip < 2 * span)
            first = tuple(jnp.where(taking, b, a) for a, b in zip(first, got))
            span *= 2
        first_other = lax.ppermute(first, "seq", swap)
        remote_keys = keys + [first[0], first_other[0]]
        remote_values = values + [first[1], first_other[1]]
    else:
        remote_keys, remote_values = keys, values

    local_flags = membership(
        listed,
        [seq_count + s, seq_count + other, s, other],
        [s >= 0, s >= 0, chip == 0, chip == 0],
    )
    local_out, local_lse = attend_partial(local_flags, query_block, keys, values, jnp.float32)

    mixed_halves = []
    for k, got_query in enumerate(got_halves):
        far_out, far_lse = attend_partial(
            got_flags, got_query, remote_keys, remote_values, jnp.bfloat16
        )
        far_out, far_lse = lax.ppermute((far_out, far_lse), "seq", forth)
        near = slice(k * half, (k + 1) * half)
        lse_a = local_lse[:, 0, near][:, :, None]
        lse_b = far_lse[:, 0, :][:, :, None]
        top = jnp.maximum(lse_a, lse_b)
        weight_a = jnp.exp(lse_a - top)
        weight_b = jnp.exp(lse_b - top)
        mixed = (
            local_out[:, near] * weight_a + far_out.astype(jnp.float32) * weight_b
        ) / (weight_a + weight_b)
        mixed_halves.append(mixed.astype(jnp.bfloat16))

    rows = queries.shape[0]
    result = jnp.zeros((rows, queries.shape[1]), jnp.bfloat16)
    for d in issue + [0]:
        start = d * rows
        piece = mixed_halves[start // half][:, start % half : start % half + rows]
        if d:
            piece = lax.ppermute(piece, "sp", [(i, (i - d) % sp_count) for i in range(sp_count)])
        piece = jnp.transpose(piece, (1, 0, 2)).reshape(rows, head_width)
        columns = ((sp_place + d) % sp_count) * head_width
        result = lax.dynamic_update_slice_in_dim(result, piece, columns, 1)
    return result


def solution(mesh):
    return jax.shard_map(
        local,
        mesh=mesh,
        in_specs=(
            P(("groups", "seq", "sp"), None),
            P(("groups", "seq"), "sp"),
            P(("groups", "seq"), "sp"),
            P(("groups", "seq"), "sp"),
            P(("groups", "seq"), "sp"),
            P(("groups", "seq"), None),
        ),
        out_specs=P(("groups", "seq", "sp"), None),
        check_vma=False,
    )
```
